256 devices in a mesh: agent: 4 (over y), tile: 64 (over x, z, core).
Axes of the slice: x: 4, y: 4, z: 8, core: 2. Of those that a mesh axis runs over, the one named last changes fastest.
Arguments:
- feats: bfloat16 [32, 256, 24, 256], P('agent', 'tile'), may hold values from -18 to 18
- types: int32 [32], replicated, may hold values from 0 to 1
- valid: int32 [32], replicated, may hold values 0 or 1
- offsets: int32 [32, 2], replicated, may hold values from -2 to 2
- w_qkv: bfloat16 [2, 256, 768], replicated, may hold values from -0.375 to 0.375
- w_out: bfloat16 [2, 256, 256], replicated, may hold values from -0.375 to 0.375
- d_out: bfloat16 [32, 256, 24, 256], P('agent', 'tile'), may hold values from -6 to 6
Outputs:
- d_feats: bfloat16 [32, 256, 24, 256], P('agent', 'tile')
- g_qkv: float32 [2, 256, 768], P(None, 'tile')
- g_out: float32 [2, 256, 256], P(None, 'tile')
The draws below stay inside these ranges and needn't reach their ends.
All inputs are finite; a program needn't handle non-finite values.
Results may differ from the reference program's by a relative error of at most 0.012.
The reference program's roundings to bfloat16 on the way count: a program that leaves them out, or rounds other values in their place, can miss the bound.
Values may be sent and summed in bfloat16 or wider, within the bound.
No kernel may reach another device: no remote copies, remote signals or barrier semaphores. Data moves between devices by JAX's collectives and lax.ppermute only.
A program may use at most 128 MiB of HBM per device.

```python
import jax
import jax.numpy as jnp
from jax import lax

C = 256
HEADS = 8
DH = 32
A_DEV = 8
AGENTS = 32
H = 256
GW = 24
MAXOFF = 2


def draw_feats(key, part):
    channel_level = jnp.arange(C, dtype=jnp.float32) / C
    normal_part = jnp.clip(jax.random.normal(key, (AGENTS, H, GW, C), jnp.float32), -6.0, 6.0)
    return (normal_part * 0.3 * jnp.power(10.0, channel_level)).astype(jnp.bfloat16)


def touch_ends(result, key, low, top_value):
    place = [jax.random.randint(jax.random.fold_in(key, axis), (), 0, length) for axis, length in enumerate(result.shape)]
    widest = result.shape.index(max(result.shape))
    next_to = place[:widest] + [(place[widest] + 1) % result.shape[widest]] + place[widest + 1:]
    return result.at[tuple(place)].set(low).at[tuple(next_to)].set(top_value)


def steps_of(own_key, extent, split, smallest, top_value):
    def one(dim, blocks):
        steps = jax.random.uniform(jax.random.fold_in(jax.random.fold_in(own_key, 6), dim), (blocks,), jnp.float32, smallest / len(split), top_value / len(split))
        return jnp.repeat(jnp.exp(steps), extent[dim] // blocks).reshape((-1,) + (1,) * (len(extent) - dim - 1))

    loudness = one(*split[0])
    for cut in split[1:]:
        loudness = loudness * one(*cut)
    return loudness


def normal_values(rng, shape, spread, limit, split=(), kind=jnp.bfloat16):
    gain = steps_of(rng, shape, split, -0.22, 0.18) if split else 1.0
    entries = jax.random.normal(rng, shape, jnp.float32) * spread * gain
    return jnp.minimum(jnp.maximum(entries, -limit), limit).astype(kind)


def setup_inputs(seed: int = 0) -> dict:
    key_list = jax.random.split(jax.random.key(seed), 8)
    feats = draw_feats(jax.random.fold_in(key_list[7], 71), 0)
    types = touch_ends(jax.random.randint(key_list[1], (AGENTS,), 0, 2), jax.random.fold_in(key_list[1], 1), 0, 1).astype(jnp.int32)
    valid = touch_ends((jax.random.randint(key_list[2], (AGENTS,), 0, 4) < 3).astype(jnp.int32), jax.random.fold_in(key_list[2], 1), 0, 1)
    offsets = touch_ends(jax.random.randint(key_list[3], (AGENTS, 2), -MAXOFF, MAXOFF + 1), jax.random.fold_in(key_list[3], 1), -MAXOFF, MAXOFF).astype(jnp.int32)
    w_qkv = normal_values(key_list[4], (2, C, 3 * C), C ** -0.5, 0.375)
    w_out = normal_values(key_list[5], (2, C, C), C ** -0.5, 0.375)
    d_out = normal_values(key_list[6], (AGENTS, H, GW, C), 1.0, 6.0, ((0, 4), (1, 64)))
    return {"feats": feats, "types": types, "valid": valid, "offsets": offsets, "w_qkv": w_qkv, "w_out": w_out, "d_out": d_out}


def relocate(field, offsets, direction):
    padded = jnp.pad(field, ((0, 0), (MAXOFF, MAXOFF), (MAXOFF, MAXOFF), (0, 0)))
    row_count = field.shape[1]
    col_count = field.shape[2]

    def pick_one(plane, offset):
        row_start = (MAXOFF + direction * offset[0]).astype(jnp.int32)
        col_start = (MAXOFF + direction * offset[1]).astype(jnp.int32)
        return lax.dynamic_slice(plane, (row_start, col_start, jnp.int32(0)), (row_count, col_count, plane.shape[2]))
    return jax.vmap(pick_one)(padded, offsets)

def reference(feats, types, valid, offsets, w_qkv, w_out, d_out):
    f32 = jnp.float32
    bf16 = jnp.bfloat16
    groups_n = AGENTS // A_DEV
    score_scale = DH ** (-0.5)
    warped = relocate(feats, offsets, 1)
    wqkv_all = jnp.take(w_qkv, types, axis=0).astype(f32)
    wout_all = jnp.take(w_out, types, axis=0).astype(f32)
    type_hot = (types[:, None] == jnp.arange(2)[None, :]).astype(f32)
    agent_ids = jnp.arange(AGENTS)
    allowed = (valid[None, :] == 1) | (agent_ids[:, None] == agent_ids[None, :])

    def one_row(totals, slices):
        row_feats, row_grads = slices
        feats_wide = row_feats.astype(f32)
        grads_wide = row_grads.astype(f32)
        qkv = jnp.einsum('agc,ace->age', feats_wide, wqkv_all).astype(bf16).astype(f32)
        query = qkv[..., :C].reshape(AGENTS, GW, HEADS, DH)
        keys = qkv[..., C:2 * C].reshape(AGENTS, GW, HEADS, DH)
        values = qkv[..., 2 * C:].reshape(AGENTS, GW, HEADS, DH)
        scores = jnp.einsum('aghd,bghd->ghab', query, keys) * score_scale
        raised = jnp.where(allowed, jnp.exp(scores), f32(0.0))
        attn_prob = raised / lax.optimization_barrier(jnp.sum(raised, axis=-1, keepdims=True))
        prob_low = attn_prob.astype(bf16).astype(f32)
        attended = jnp.einsum('ghab,bghd->aghd', prob_low, values).astype(bf16).astype(f32).reshape(AGENTS, GW, C)
        d_attended = jnp.einsum('age,ace->agc', grads_wide, wout_all).astype(bf16).astype(f32)
        raw_out = jnp.einsum('at,agc,age->tce', type_hot, attended, grads_wide)
        attended_heads = d_attended.reshape(AGENTS, GW, HEADS, DH)
        prob_grad = jnp.einsum('aghd,bghd->ghab', attended_heads, values)
        score_grad = (attn_prob * (prob_grad - lax.optimization_barrier(jnp.sum(attn_prob * prob_grad, axis=-1, keepdims=True))) * score_scale).astype(bf16).astype(f32)
        d_query = jnp.einsum('ghab,bghd->aghd', score_grad, keys).astype(bf16).astype(f32).reshape(AGENTS, GW, C)
        grad_blocks = score_grad.reshape(GW, HEADS, groups_n, A_DEV, AGENTS)
        prob_blocks = prob_low.reshape(GW, HEADS, groups_n, A_DEV, AGENTS)
        query_blocks = query.reshape(groups_n, A_DEV, GW, HEADS, DH)
        dattn_blocks = attended_heads.reshape(groups_n, A_DEV, GW, HEADS, DH)
        key_parts = jnp.einsum('ghnyb,nyghd->nbghd', grad_blocks, query_blocks).astype(bf16).astype(f32)
        value_parts = jnp.einsum('ghnyb,nyghd->nbghd', prob_blocks, dattn_blocks).astype(bf16).astype(f32)
        key_sum = lax.optimization_barrier(jnp.sum(key_parts, axis=0)).reshape(AGENTS, GW, C)
        value_sum = lax.optimization_barrier(jnp.sum(value_parts, axis=0)).reshape(AGENTS, GW, C)
        d_qkv = jnp.concatenate([d_query, key_sum, value_sum], axis=-1)
        d_warped = jnp.einsum('bge,bce->bgc', d_qkv, wqkv_all).astype(bf16)
        raw_qkv = jnp.einsum('bt,bgc,bge->tce', type_hot, feats_wide, d_qkv)
        return ((totals[0] + raw_qkv, totals[1] + raw_out), d_warped)
    start_totals = (jnp.zeros((2, C, 3 * C), f32), jnp.zeros((2, C, C), f32))
    rows_in = (jnp.transpose(warped, (1, 0, 2, 3)), jnp.transpose(d_out, (1, 0, 2, 3)))
    totals, stacked = lax.scan(one_row, start_totals, rows_in)
    d_warped = jnp.transpose(stacked, (1, 0, 2, 3))
    d_feats = relocate(d_warped, offsets, -1)
    raw_qkv, raw_out = totals
    norm_value = jnp.sqrt(jnp.sum(raw_qkv * raw_qkv) + jnp.sum(raw_out * raw_out))
    norm_limit = jnp.sqrt(f32(8.0 * C * C))
    factor = norm_limit / jnp.maximum(norm_value, norm_limit)
    return (d_feats, raw_qkv * factor, raw_out * factor)
```

```python
import math

import jax
import jax.numpy as jnp
from jax import lax
from jax.sharding import PartitionSpec as P

HEADS = 8
MAXOFF = 2


def with_halo(cells, sides, width):
    for axis, dim in sides:
        count = lax.axis_size(axis)
        ends = count - 1
        head = lax.slice_in_dim(cells, 0, width, axis=dim)
        tail = lax.slice_in_dim(cells, cells.shape[dim] - width, cells.shape[dim], axis=dim)
        cells = jnp.concatenate(
            [
                lax.ppermute(tail, axis, [(i, (i + 1) % count) for i in range(ends)]),
                cells,
                lax.ppermute(head, axis, [((i + 1) % count, i) for i in range(ends)]),
            ],
            axis=dim,
        )
    return cells


def relocate(rimmed, offsets, direction):
    padded = jnp.pad(rimmed, ((0, 0), (0, 0), (MAXOFF, MAXOFF), (0, 0)))
    row_count = rimmed.shape[1] - 2 * MAXOFF
    col_count = rimmed.shape[2]

    def pick_one(plane, offset):
        row_start = MAXOFF + direction * offset[0]
        col_start = MAXOFF + direction * offset[1]
        return lax.dynamic_slice(
            plane, (row_start, col_start, jnp.int32(0)), (row_count, col_count, plane.shape[2])
        )

    return jax.vmap(pick_one)(padded, offsets)


def body(feats, types, valid, offsets, w_qkv, w_out, d_out):
    f32 = jnp.float32
    bf16 = jnp.bfloat16
    highest = lax.Precision.HIGHEST
    own_count, row_count, col_count, channels = feats.shape
    agents = own_count * lax.axis_size("agent")
    first_agent = lax.axis_index("agent") * own_count
    own_offsets = lax.dynamic_slice_in_dim(offsets, first_agent, own_count, 0)
    rimmed = with_halo(feats, (("tile", 1),), MAXOFF)
    warped = relocate(rimmed, own_offsets, 1)
    cell_count = row_count * col_count
    head_size = channels // HEADS
    score_scale = head_size ** (-0.5)
    all_hot = (types[:, None] == jnp.arange(2)[None, :]).astype(bf16)
    flat_feats = warped.reshape(own_count, cell_count, channels)
    flat_grads = d_out.reshape(own_count, cell_count, channels)
    all_feats, all_grads = (
        lax.all_to_all(flat_feats, "agent", split_axis=1, concat_axis=0, tiled=True),
        lax.all_to_all(flat_grads, "agent", split_axis=1, concat_axis=0, tiled=True),
    )
    part_cells = all_feats.shape[1]
    pairs = agents * part_cells
    is_type1 = (types == 1)[:, None, None]
    type_mask = jnp.stack([types == 0, types == 1], axis=0)[:, :, None, None]
    feats_rows = all_feats.reshape(pairs, channels)
    grads_rows = all_grads.reshape(pairs, channels)
    qkv_both = jnp.einsum(
        "pc,tce->tpe", feats_rows, w_qkv, preferred_element_type=f32
    ).astype(bf16).reshape(2, agents, part_cells, 3 * channels)
    qkv = jnp.where(is_type1, qkv_both[1], qkv_both[0])
    query_heads = qkv[..., :channels].reshape(agents, part_cells, HEADS, head_size)
    key_heads = qkv[..., channels : 2 * channels].reshape(agents, part_cells, HEADS, head_size)
    value_heads = qkv[..., 2 * channels :].reshape(agents, part_cells, HEADS, head_size)
    scores = (
        jnp.einsum("aghd,bghd->ghab", query_heads, key_heads, preferred_element_type=f32)
        * score_scale
    )
    agent_ids = jnp.arange(agents)
    allowed = (valid[None, :] == 1) | (agent_ids[:, None] == agent_ids[None, :])
    raised = jnp.where(allowed, jnp.exp(scores), f32(0.0))
    attn_prob = raised / jnp.sum(raised, axis=-1, keepdims=True)
    prob_low = attn_prob.astype(bf16)
    attended = (
        jnp.einsum("ghab,bghd->aghd", prob_low, value_heads, preferred_element_type=f32)
        .astype(bf16)
        .reshape(agents, part_cells, channels)
    )
    d_att_both = jnp.einsum(
        "pe,tce->tpc", grads_rows, w_out, preferred_element_type=f32
    ).astype(bf16).reshape(2, agents, part_cells, channels)
    d_attended = jnp.where(is_type1, d_att_both[1], d_att_both[0])
    attended_typed = jnp.where(type_mask, attended[None], jnp.zeros((), bf16))
    raw_out = jnp.einsum(
        "tpc,pe->tce",
        attended_typed.reshape(2, pairs, channels),
        grads_rows,
        preferred_element_type=f32,
    )
    attended_heads = d_attended.reshape(agents, part_cells, HEADS, head_size)
    prob_grad = jnp.einsum(
        "aghd,bghd->ghab", attended_heads, value_heads, preferred_element_type=f32
    )
    score_grad = (
        attn_prob
        * (prob_grad - jnp.sum(attn_prob * prob_grad, axis=-1, keepdims=True))
        * score_scale
    ).astype(bf16)
    d_query = (
        jnp.einsum("ghab,bghd->aghd", score_grad, key_heads, preferred_element_type=f32)
        .astype(bf16)
        .reshape(agents, part_cells, channels)
    )
    groups_n = agents // own_count
    grad_blocks = score_grad.reshape(part_cells, HEADS, groups_n, own_count, agents)
    prob_blocks = prob_low.reshape(part_cells, HEADS, groups_n, own_count, agents)
    query_blocks = query_heads.reshape(groups_n, own_count, part_cells, HEADS, head_size)
    dattn_blocks = attended_heads.reshape(groups_n, own_count, part_cells, HEADS, head_size)
    key_parts = jnp.einsum(
        "ghnyb,nyghd->nbghd", grad_blocks, query_blocks, preferred_element_type=f32
    ).astype(bf16)
    value_parts = jnp.einsum(
        "ghnyb,nyghd->nbghd", prob_blocks, dattn_blocks, preferred_element_type=f32
    ).astype(bf16)
    key_sum = jnp.sum(key_parts.astype(f32), axis=0).reshape(agents, part_cells, channels)
    value_sum = jnp.sum(value_parts.astype(f32), axis=0).reshape(agents, part_cells, channels)
    d_qkv = jnp.concatenate([d_query.astype(f32), key_sum, value_sum], axis=-1)
    d_hi = d_qkv.astype(bf16)
    d_lo = (d_qkv - d_hi.astype(f32)).astype(bf16)
    d_split = jnp.stack([d_hi, d_lo], axis=0).reshape(2, pairs, 3 * channels)
    d_part_terms = jnp.einsum(
        "spe,tce->stpc", d_split, w_qkv, preferred_element_type=f32
    )
    d_part_sum = (d_part_terms[0] + d_part_terms[1]).reshape(2, agents, part_cells, channels)
    d_part = jnp.where(is_type1, d_part_sum[1], d_part_sum[0]).astype(bf16)
    returned = lax.all_to_all(d_part, "agent", split_axis=0, concat_axis=1, tiled=True)
    d_warped = returned.reshape(own_count, row_count, col_count, channels)
    feats_typed = jnp.where(type_mask, all_feats[None], jnp.zeros((), bf16)).reshape(
        2, pairs, channels
    )
    qkv_terms = jnp.einsum(
        "tpc,spe->stce", feats_typed, d_split, preferred_element_type=f32
    )
    raw_qkv = qkv_terms[0] + qkv_terms[1]
    rimmed_grad = with_halo(d_warped, (("tile", 1),), MAXOFF)
    d_feats = relocate(rimmed_grad, own_offsets, -1)
    norm_limit = math.sqrt(8.0 * channels * channels)
    raw_all = jnp.concatenate([raw_qkv, raw_out], axis=-1)
    share_all = lax.psum_scatter(raw_all, "tile", scatter_dimension=1, tiled=True)
    share_all = lax.psum(share_all, "agent")
    square_sum = lax.psum(jnp.sum(share_all * share_all), "tile")
    factor = norm_limit / jnp.maximum(jnp.sqrt(square_sum), norm_limit)
    scaled = share_all * factor
    return (d_feats, scaled[..., : 3 * channels], scaled[..., 3 * channels :])


def solution(mesh):
    placed = (
        P("agent", "tile", None, None),
        P(),
        P(),
        P(),
        P(),
        P(),
        P("agent", "tile", None, None),
    )
    return jax.shard_map(
        body,
        mesh=mesh,
        in_specs=placed,
        out_specs=(P("agent", "tile", None, None), P(None, "tile", None), P(None, "tile", None)),
        check_vma=False,
    )
```

```python
import math

import jax
import jax.numpy as jnp
from jax import lax
from jax.sharding import PartitionSpec as P

HEADS = 8
MAXOFF = 2


def axis_bits(axis):
    count = lax.axis_size(axis)
    bits = count.bit_length() - 1
    assert 1 << bits == count
    return bits


def xor_pairs(count, bit):
    return [(i, i ^ (1 << bit)) for i in range(count)]


def tile_bit_order(count):
    bits = count.bit_length() - 1
    preferred = [0, 1, 4, 2, 5, 3]
    return [b for b in preferred if b < bits] + [b for b in range(bits) if b not in preferred]


def halving_sum(pieces, axis, bit_order):
    count = lax.axis_size(axis)
    me = lax.axis_index(axis)
    bits = axis_bits(axis)
    rest = pieces.shape[1:]
    x = pieces.reshape((2,) * bits + rest)
    for bit in bit_order:
        dim = bits - 1 - bit
        mine = (me >> bit) & 1
        low = lax.index_in_dim(x, 0, dim, keepdims=True)
        high = lax.index_in_dim(x, 1, dim, keepdims=True)
        keep = jnp.where(mine == 1, high, low)
        send = jnp.where(mine == 1, low, high)
        x = keep + lax.ppermute(send, axis, xor_pairs(count, bit))
    return x.reshape(rest)


def doubling_sum(x, axis, bit_order):
    count = lax.axis_size(axis)
    for bit in bit_order:
        x = x + lax.ppermute(x, axis, xor_pairs(count, bit))
    return x


def with_halo(cells, sides, width):
    for axis, dim in sides:
        count = lax.axis_size(axis)
        ends = count - 1
        head = lax.slice_in_dim(cells, 0, width, axis=dim)
        tail = lax.slice_in_dim(cells, cells.shape[dim] - width, cells.shape[dim], axis=dim)
        cells = jnp.concatenate(
            [
                lax.ppermute(tail, axis, [(i, (i + 1) % count) for i in range(ends)]),
                cells,
                lax.ppermute(head, axis, [((i + 1) % count, i) for i in range(ends)]),
            ],
            axis=dim,
        )
    return cells


def relocate(rimmed, offsets, direction):
    padded = jnp.pad(rimmed, ((0, 0), (0, 0), (MAXOFF, MAXOFF), (0, 0)))
    row_count = rimmed.shape[1] - 2 * MAXOFF
    col_count = rimmed.shape[2]

    def pick_one(plane, offset):
        row_start = MAXOFF + direction * offset[0]
        col_start = MAXOFF + direction * offset[1]
        return lax.dynamic_slice(
            plane, (row_start, col_start, jnp.int32(0)), (row_count, col_count, plane.shape[2])
        )

    return jax.vmap(pick_one)(padded, offsets)


def body(feats, types, valid, offsets, w_qkv, w_out, d_out):
    f32 = jnp.float32
    bf16 = jnp.bfloat16
    highest = lax.Precision.HIGHEST
    own_count, row_count, col_count, channels = feats.shape
    agents = own_count * lax.axis_size("agent")
    first_agent = lax.axis_index("agent") * own_count
    own_offsets = lax.dynamic_slice_in_dim(offsets, first_agent, own_count, 0)
    rimmed = with_halo(feats, (("tile", 1),), MAXOFF)
    warped = relocate(rimmed, own_offsets, 1)
    cell_count = row_count * col_count
    head_size = channels // HEADS
    score_scale = head_size ** (-0.5)
    all_hot = (types[:, None] == jnp.arange(2)[None, :]).astype(bf16)
    flat_feats = warped.reshape(own_count, cell_count, channels)
    flat_grads = d_out.reshape(own_count, cell_count, channels)
    all_feats, all_grads = (
        lax.all_to_all(flat_feats, "agent", split_axis=1, concat_axis=0, tiled=True),
        lax.all_to_all(flat_grads, "agent", split_axis=1, concat_axis=0, tiled=True),
    )
    part_cells = all_feats.shape[1]
    pairs = agents * part_cells
    is_type1 = (types == 1)[:, None, None]
    type_mask = jnp.stack([types == 0, types == 1], axis=0)[:, :, None, None]
    feats_rows = all_feats.reshape(pairs, channels)
    grads_rows = all_grads.reshape(pairs, channels)
    qkv_both = jnp.einsum(
        "pc,tce->tpe", feats_rows, w_qkv, preferred_element_type=f32
    ).astype(bf16).reshape(2, agents, part_cells, 3 * channels)
    qkv = jnp.where(is_type1, qkv_both[1], qkv_both[0])
    query_heads = qkv[..., :channels].reshape(agents, part_cells, HEADS, head_size)
    key_heads = qkv[..., channels : 2 * channels].reshape(agents, part_cells, HEADS, head_size)
    value_heads = qkv[..., 2 * channels :].reshape(agents, part_cells, HEADS, head_size)
    scores = (
        jnp.einsum("aghd,bghd->ghab", query_heads, key_heads, preferred_element_type=f32)
        * score_scale
    )
    agent_ids = jnp.arange(agents)
    allowed = (valid[None, :] == 1) | (agent_ids[:, None] == agent_ids[None, :])
    raised = jnp.where(allowed, jnp.exp(scores), f32(0.0))
    attn_prob = raised / jnp.sum(raised, axis=-1, keepdims=True)
    prob_low = attn_prob.astype(bf16)
    attended = (
        jnp.einsum("ghab,bghd->aghd", prob_low, value_heads, preferred_element_type=f32)
        .astype(bf16)
        .reshape(agents, part_cells, channels)
    )
    d_att_both = jnp.einsum(
        "pe,tce->tpc", grads_rows, w_out, preferred_element_type=f32
    ).astype(bf16).reshape(2, agents, part_cells, channels)
    d_attended = jnp.where(is_type1, d_att_both[1], d_att_both[0])
    attended_typed = jnp.where(type_mask, attended[None], jnp.zeros((), bf16))
    raw_out = jnp.einsum(
        "tpc,pe->tce",
        attended_typed.reshape(2, pairs, channels),
        grads_rows,
        preferred_element_type=f32,
    )
    attended_heads = d_attended.reshape(agents, part_cells, HEADS, head_size)
    prob_grad = jnp.einsum(
        "aghd,bghd->ghab", attended_heads, value_heads, preferred_element_type=f32
    )
    score_grad = (
        attn_prob
        * (prob_grad - jnp.sum(attn_prob * prob_grad, axis=-1, keepdims=True))
        * score_scale
    ).astype(bf16)
    d_query = (
        jnp.einsum("ghab,bghd->aghd", score_grad, key_heads, preferred_element_type=f32)
        .astype(bf16)
        .reshape(agents, part_cells, channels)
    )
    groups_n = agents // own_count
    grad_blocks = score_grad.reshape(part_cells, HEADS, groups_n, own_count, agents)
    prob_blocks = prob_low.reshape(part_cells, HEADS, groups_n, own_count, agents)
    query_blocks = query_heads.reshape(groups_n, own_count, part_cells, HEADS, head_size)
    dattn_blocks = attended_heads.reshape(groups_n, own_count, part_cells, HEADS, head_size)
    key_parts = jnp.einsum(
        "ghnyb,nyghd->nbghd", grad_blocks, query_blocks, preferred_element_type=f32
    ).astype(bf16)
    value_parts = jnp.einsum(
        "ghnyb,nyghd->nbghd", prob_blocks, dattn_blocks, preferred_element_type=f32
    ).astype(bf16)
    key_sum = jnp.sum(key_parts.astype(f32), axis=0).reshape(agents, part_cells, channels)
    value_sum = jnp.sum(value_parts.astype(f32), axis=0).reshape(agents, part_cells, channels)
    d_qkv = jnp.concatenate([d_query.astype(f32), key_sum, value_sum], axis=-1)
    d_hi = d_qkv.astype(bf16)
    d_lo = (d_qkv - d_hi.astype(f32)).astype(bf16)
    d_split = jnp.stack([d_hi, d_lo], axis=0).reshape(2, pairs, 3 * channels)
    d_part_terms = jnp.einsum(
        "spe,tce->stpc", d_split, w_qkv, preferred_element_type=f32
    )
    d_part_sum = (d_part_terms[0] + d_part_terms[1]).reshape(2, agents, part_cells, channels)
    d_part = jnp.where(is_type1, d_part_sum[1], d_part_sum[0]).astype(bf16)
    returned = lax.all_to_all(d_part, "agent", split_axis=0, concat_axis=1, tiled=True)
    d_warped = returned.reshape(own_count, row_count, col_count, channels)
    feats_typed = jnp.where(type_mask, all_feats[None], jnp.zeros((), bf16)).reshape(
        2, pairs, channels
    )
    qkv_terms = jnp.einsum(
        "tpc,spe->stce", feats_typed, d_split, preferred_element_type=f32
    )
    raw_qkv = qkv_terms[0] + qkv_terms[1]
    rimmed_grad = with_halo(d_warped, (("tile", 1),), MAXOFF)
    d_feats = relocate(rimmed_grad, own_offsets, -1)
    norm_limit = math.sqrt(8.0 * channels * channels)
    raw_all = jnp.concatenate([raw_qkv, raw_out], axis=-1)
    tiles = lax.axis_size("tile")
    share_rows = channels // tiles
    pieces = raw_all.reshape(2, tiles, share_rows, 4 * channels).transpose(1, 0, 2, 3)
    share_all = halving_sum(pieces, "tile", tile_bit_order(tiles))
    share_all = doubling_sum(share_all, "agent", list(range(axis_bits("agent"))))
    square_sum = jnp.broadcast_to(jnp.sum(share_all * share_all), (8, 128))
    square_sum = doubling_sum(square_sum, "tile", list(range(axis_bits("tile"))))[0, 0]
    factor = norm_limit / jnp.maximum(jnp.sqrt(square_sum), norm_limit)
    scaled = share_all * factor
    return (d_feats, scaled[..., : 3 * channels], scaled[..., 3 * channels :])


def solution(mesh):
    placed = (
        P("agent", "tile", None, None),
        P(),
        P(),
        P(),
        P(),
        P(),
        P("agent", "tile", None, None),
    )
    return jax.shard_map(
        body,
        mesh=mesh,
        in_specs=placed,
        out_specs=(P("agent", "tile", None, None), P(None, "tile", None), P(None, "tile", None)),
        check_vma=False,
    )
```

```python
import functools
import math

import jax
import jax.numpy as jnp
from jax import lax
from jax.experimental import pallas as pl
from jax.sharding import PartitionSpec as P

HEADS = 8
MAXOFF = 2


def axis_bits(axis):
    count = lax.axis_size(axis)
    bits = count.bit_length() - 1
    assert 1 << bits == count
    return bits


def xor_pairs(count, bit):
    return [(i, i ^ (1 << bit)) for i in range(count)]


def tile_bit_order(count):
    bits = count.bit_length() - 1
    preferred = [0, 1, 4, 2, 5, 3]
    return [b for b in preferred if b < bits] + [b for b in range(bits) if b not in preferred]


def halving_sum(pieces, axis, bit_order):
    count = lax.axis_size(axis)
    me = lax.axis_index(axis)
    bits = axis_bits(axis)
    rest = pieces.shape[1:]
    x = pieces.reshape((2,) * bits + rest)
    for bit in bit_order:
        dim = bits - 1 - bit
        mine = (me >> bit) & 1
        low = lax.index_in_dim(x, 0, dim, keepdims=True)
        high = lax.index_in_dim(x, 1, dim, keepdims=True)
        keep = jnp.where(mine == 1, high, low)
        send = jnp.where(mine == 1, low, high)
        x = keep + lax.ppermute(send, axis, xor_pairs(count, bit))
    return x.reshape(rest)


def doubling_sum(x, axis, bit_order):
    count = lax.axis_size(axis)
    for bit in bit_order:
        x = x + lax.ppermute(x, axis, xor_pairs(count, bit))
    return x


def with_halo(cells, sides, width):
    for axis, dim in sides:
        count = lax.axis_size(axis)
        ends = count - 1
        head = lax.slice_in_dim(cells, 0, width, axis=dim)
        tail = lax.slice_in_dim(cells, cells.shape[dim] - width, cells.shape[dim], axis=dim)
        cells = jnp.concatenate(
            [
                lax.ppermute(tail, axis, [(i, (i + 1) % count) for i in range(ends)]),
                cells,
                lax.ppermute(head, axis, [((i + 1) % count, i) for i in range(ends)]),
            ],
            axis=dim,
        )
    return cells


def relocate(rimmed, offsets, direction):
    padded = jnp.pad(rimmed, ((0, 0), (0, 0), (MAXOFF, MAXOFF), (0, 0)))
    row_count = rimmed.shape[1] - 2 * MAXOFF
    col_count = rimmed.shape[2]

    def pick_one(plane, offset):
        row_start = MAXOFF + direction * offset[0]
        col_start = MAXOFF + direction * offset[1]
        return lax.dynamic_slice(
            plane, (row_start, col_start, jnp.int32(0)), (row_count, col_count, plane.shape[2])
        )

    return jax.vmap(pick_one)(padded, offsets)


def attention_kernel(block_size, valid_ref, qkv_ref, da_ref, att_ref, split_ref):
    f32 = jnp.float32
    bf16 = jnp.bfloat16
    cells, agents, channels = da_ref.shape
    head_size = channels // HEADS
    blocks = agents // block_size
    rows = blocks * HEADS * block_size
    scale = head_size ** (-0.5)
    dims_nt = (((1,), (1,)), ((), ()))
    dims_tn = (((0,), (0,)), ((), ()))
    lane = lax.broadcasted_iota(jnp.int32, (HEADS, channels), 1)
    head = lax.broadcasted_iota(jnp.int32, (HEADS, channels), 0)
    head_mask = (lane // head_size == head).astype(f32).reshape(1, HEADS, 1, channels)
    row_id = lax.broadcasted_iota(jnp.int32, (rows, agents), 0)
    col_id = lax.broadcasted_iota(jnp.int32, (rows, agents), 1)
    row_agent = (row_id // (HEADS * block_size)) * block_size + row_id % block_size
    allowed = (valid_ref[...] > 0.5) | (row_agent == col_id)

    def stack(x):
        spread = x.astype(f32).reshape(blocks, 1, block_size, channels) * head_mask
        return spread.reshape(rows, channels).astype(bf16)

    def unstack(y):
        return jnp.sum(y.reshape(blocks, HEADS, block_size, channels) * head_mask, axis=1).reshape(
            agents, channels
        )

    def one_cell(c, carry):
        q = qkv_ref[c, :, 0:channels]
        k = qkv_ref[c, :, channels : 2 * channels]
        v = qkv_ref[c, :, 2 * channels : 3 * channels]
        q_rows = stack(q)
        da_rows = stack(da_ref[c])
        scores = lax.dot_general(q_rows, k, dims_nt, preferred_element_type=f32) * scale
        raised = jnp.where(allowed, jnp.exp(scores), f32(0.0))
        prob = raised / jnp.sum(raised, axis=1, keepdims=True)
        prob_low = prob.astype(bf16)
        att = unstack(jnp.dot(prob_low, v, preferred_element_type=f32))
        att_ref[c] = att.astype(bf16)
        prob_grad = lax.dot_general(da_rows, v, dims_nt, preferred_element_type=f32)
        score_grad = (
            prob * (prob_grad - jnp.sum(prob * prob_grad, axis=1, keepdims=True)) * scale
        ).astype(bf16)
        d_q = unstack(jnp.dot(score_grad, k, preferred_element_type=f32)).astype(bf16).astype(f32)
        d_k = jnp.zeros((agents, channels), f32)
        d_v = jnp.zeros((agents, channels), f32)
        for n in range(blocks):
            part = slice(n * HEADS * block_size, (n + 1) * HEADS * block_size)
            d_k = d_k + lax.dot_general(
                score_grad[part], q_rows[part], dims_tn, preferred_element_type=f32
            ).astype(bf16).astype(f32)
            d_v = d_v + lax.dot_general(
                prob_low[part], da_rows[part], dims_tn, preferred_element_type=f32
            ).astype(bf16).astype(f32)
        for i, d in enumerate((d_q, d_k, d_v)):
            hi = d.astype(bf16)
            split_ref[0, c, :, i * channels : (i + 1) * channels] = hi
            split_ref[1, c, :, i * channels : (i + 1) * channels] = (d - hi.astype(f32)).astype(bf16)
        return carry

    lax.fori_loop(0, cells, one_cell, 0)


def cell_attention(valid_row, qkv, d_attended, block_size):
    cells, agents, channels = d_attended.shape
    step = 4 if cells % 4 == 0 else 1
    return pl.pallas_call(
        functools.partial(attention_kernel, block_size),
        grid=(cells // step,),
        in_specs=[
            pl.BlockSpec((1, agents), lambda i: (0, 0)),
            pl.BlockSpec((step, agents, 3 * channels), lambda i: (i, 0, 0)),
            pl.BlockSpec((step, agents, channels), lambda i: (i, 0, 0)),
        ],
        out_specs=[
            pl.BlockSpec((step, agents, channels), lambda i: (i, 0, 0)),
            pl.BlockSpec((2, step, agents, 3 * channels), lambda i: (0, i, 0, 0)),
        ],
        out_shape=[
            jax.ShapeDtypeStruct((cells, agents, channels), jnp.bfloat16),
            jax.ShapeDtypeStruct((2, cells, agents, 3 * channels), jnp.bfloat16),
        ],
        cost_estimate=pl.CostEstimate(
            flops=cells * 48 * agents * HEADS * agents * channels,
            transcendentals=cells * agents * HEADS * agents,
            bytes_accessed=cells * agents * channels * 2 * 11,
        ),
    )(valid_row, qkv, d_attended)


def body(feats, types, valid, offsets, w_qkv, w_out, d_out):
    f32 = jnp.float32
    bf16 = jnp.bfloat16
    highest = lax.Precision.HIGHEST
    own_count, row_count, col_count, channels = feats.shape
    agents = own_count * lax.axis_size("agent")
    first_agent = lax.axis_index("agent") * own_count
    own_offsets = lax.dynamic_slice_in_dim(offsets, first_agent, own_count, 0)
    rimmed = with_halo(feats, (("tile", 1),), MAXOFF)
    warped = relocate(rimmed, own_offsets, 1)
    cell_count = row_count * col_count
    head_size = channels // HEADS
    score_scale = head_size ** (-0.5)
    all_hot = (types[:, None] == jnp.arange(2)[None, :]).astype(bf16)
    flat_feats = warped.reshape(own_count, cell_count, channels)
    flat_grads = d_out.reshape(own_count, cell_count, channels)
    all_feats, all_grads = (
        lax.all_to_all(flat_feats, "agent", split_axis=1, concat_axis=0, tiled=True),
        lax.all_to_all(flat_grads, "agent", split_axis=1, concat_axis=0, tiled=True),
    )
    part_cells = all_feats.shape[1]
    pairs = agents * part_cells
    is_type1 = (types == 1)[None, :, None]
    type_mask = jnp.stack([types == 0, types == 1], axis=0)[:, None, :, None]
    feats_cm = jnp.transpose(all_feats, (1, 0, 2))
    grads_cm = jnp.transpose(all_grads, (1, 0, 2))
    qkv_both = jnp.einsum(
        "gac,tce->tgae", feats_cm, w_qkv, preferred_element_type=f32
    ).astype(bf16)
    qkv = jnp.where(is_type1, qkv_both[1], qkv_both[0])
    d_att_both = jnp.einsum(
        "gae,tce->tgac", grads_cm, w_out, preferred_element_type=f32
    ).astype(bf16)
    d_attended = jnp.where(is_type1, d_att_both[1], d_att_both[0])
    valid_row = (valid == 1).astype(f32).reshape(1, agents)
    attended, d_split = cell_attention(valid_row, qkv, d_attended, own_count)
    attended_typed = jnp.where(type_mask, attended[None], jnp.zeros((), bf16))
    raw_out = jnp.einsum(
        "tgac,gae->tce", attended_typed, grads_cm, preferred_element_type=f32
    )
    d_part_terms = jnp.einsum(
        "sgae,tce->stgac", d_split, w_qkv, preferred_element_type=f32
    )
    d_part_sum = d_part_terms[0] + d_part_terms[1]
    d_part = jnp.where(is_type1, d_part_sum[1], d_part_sum[0]).astype(bf16)
    d_part = jnp.transpose(d_part, (1, 0, 2))
    returned = lax.all_to_all(d_part, "agent", split_axis=0, concat_axis=1, tiled=True)
    d_warped = returned.reshape(own_count, row_count, col_count, channels)
    feats_typed = jnp.where(type_mask, feats_cm[None], jnp.zeros((), bf16))
    qkv_terms = jnp.einsum(
        "tgac,sgae->stce", feats_typed, d_split, preferred_element_type=f32
    )
    raw_qkv = qkv_terms[0] + qkv_terms[1]
    rimmed_grad = with_halo(d_warped, (("tile", 1),), MAXOFF)
    d_feats = relocate(rimmed_grad, own_offsets, -1)
    norm_limit = math.sqrt(8.0 * channels * channels)
    raw_all = jnp.concatenate([raw_qkv, raw_out], axis=-1)
    tiles = lax.axis_size("tile")
    share_rows = channels // tiles
    pieces = raw_all.reshape(2, tiles, share_rows, 4 * channels).transpose(1, 0, 2, 3)
    share_all = halving_sum(pieces, "tile", tile_bit_order(tiles))
    share_all = doubling_sum(share_all, "agent", list(range(axis_bits("agent"))))
    square_sum = jnp.broadcast_to(jnp.sum(share_all * share_all), (8, 128))
    square_sum = doubling_sum(square_sum, "tile", list(range(axis_bits("tile"))))[0, 0]
    factor = norm_limit / jnp.maximum(jnp.sqrt(square_sum), norm_limit)
    scaled = share_all * factor
    return (d_feats, scaled[..., : 3 * channels], scaled[..., 3 * channels :])


def solution(mesh):
    placed = (
        P("agent", "tile", None, None),
        P(),
        P(),
        P(),
        P(),
        P(),
        P("agent", "tile", None, None),
    )
    return jax.shard_map(
        body,
        mesh=mesh,
        in_specs=placed,
        out_specs=(P("agent", "tile", None, None), P(None, "tile", None), P(None, "tile", None)),
        check_vma=False,
    )
```

```python
import functools
import math

import jax
import jax.numpy as jnp
from jax import lax
from jax.experimental import pallas as pl
from jax.sharding import PartitionSpec as P

HEADS = 8
MAXOFF = 2


def axis_bits(axis):
    count = lax.axis_size(axis)
    bits = count.bit_length() - 1
    assert 1 << bits == count
    return bits


def xor_pairs(count, bit):
    return [(i, i ^ (1 << bit)) for i in range(count)]


def tile_bit_order(count):
    bits = count.bit_length() - 1
    preferred = [0, 1, 4, 2, 5, 3]
    return [b for b in preferred if b < bits] + [b for b in range(bits) if b not in preferred]


def halving_sum(pieces, axis, bit_order):
    count = lax.axis_size(axis)
    me = lax.axis_index(axis)
    bits = axis_bits(axis)
    rest = pieces.shape[1:]
    x = pieces.reshape((2,) * bits + rest)
    for bit in bit_order:
        dim = bits - 1 - bit
        mine = (me >> bit) & 1
        low = lax.index_in_dim(x, 0, dim, keepdims=True)
        high = lax.index_in_dim(x, 1, dim, keepdims=True)
        keep = jnp.where(mine == 1, high, low)
        send = jnp.where(mine == 1, low, high)
        x = keep + lax.ppermute(send, axis, xor_pairs(count, bit))
    return x.reshape(rest)


def doubling_sum(x, axis, bit_order):
    count = lax.axis_size(axis)
    for bit in bit_order:
        x = x + lax.ppermute(x, axis, xor_pairs(count, bit))
    return x


def with_halo(cells, sides, width):
    for axis, dim in sides:
        count = lax.axis_size(axis)
        ends = count - 1
        head = lax.slice_in_dim(cells, 0, width, axis=dim)
        tail = lax.slice_in_dim(cells, cells.shape[dim] - width, cells.shape[dim], axis=dim)
        cells = jnp.concatenate(
            [
                lax.ppermute(tail, axis, [(i, (i + 1) % count) for i in range(ends)]),
                cells,
                lax.ppermute(head, axis, [((i + 1) % count, i) for i in range(ends)]),
            ],
            axis=dim,
        )
    return cells


def relocate(rimmed, offsets, direction):
    padded = jnp.pad(rimmed, ((0, 0), (0, 0), (MAXOFF, MAXOFF), (0, 0)))
    row_count = rimmed.shape[1] - 2 * MAXOFF
    col_count = rimmed.shape[2]

    def pick_one(plane, offset):
        row_start = MAXOFF + direction * offset[0]
        col_start = MAXOFF + direction * offset[1]
        return lax.dynamic_slice(
            plane, (row_start, col_start, jnp.int32(0)), (row_count, col_count, plane.shape[2])
        )

    return jax.vmap(pick_one)(padded, offsets)


def attention_kernel(block_size, valid_ref, qkv_ref, da_ref, att_ref, split_ref):
    f32 = jnp.float32
    bf16 = jnp.bfloat16
    cells, agents, channels = da_ref.shape
    head_size = channels // HEADS
    blocks = agents // block_size
    rows = blocks * HEADS * block_size
    scale = head_size ** (-0.5)
    dims_nt = (((1,), (1,)), ((), ()))
    dims_tn = (((0,), (0,)), ((), ()))
    lane = lax.broadcasted_iota(jnp.int32, (HEADS, channels), 1)
    head = lax.broadcasted_iota(jnp.int32, (HEADS, channels), 0)
    head_mask = (lane // head_size == head).astype(f32).reshape(1, HEADS, 1, channels)
    key_id = lax.broadcasted_iota(jnp.int32, (agents, rows), 0)
    row_id = lax.broadcasted_iota(jnp.int32, (agents, rows), 1)
    row_agent = (row_id // (HEADS * block_size)) * block_size + row_id % block_size
    allowed = (valid_ref[...] > 0.5) | (row_agent == key_id)
    row_block = row_id // (HEADS * block_size)

    def stack(x):
        spread = x.astype(f32).reshape(blocks, 1, block_size, channels) * head_mask
        return spread.reshape(rows, channels).astype(bf16)

    def unstack(y):
        return jnp.sum(y.reshape(blocks, HEADS, block_size, channels) * head_mask, axis=1).reshape(
            agents, channels
        )

    def one_cell(c, carry):
        q = qkv_ref[c, :, 0:channels]
        k = qkv_ref[c, :, channels : 2 * channels]
        v = qkv_ref[c, :, 2 * channels : 3 * channels]
        q_rows = stack(q)
        da_rows = stack(da_ref[c])
        scores = lax.dot_general(k, q_rows, dims_nt, preferred_element_type=f32) * scale
        raised = jnp.where(allowed, jnp.exp(scores), f32(0.0))
        prob = raised / jnp.sum(raised, axis=0, keepdims=True)
        prob_low = prob.astype(bf16)
        att = unstack(lax.dot_general(prob_low, v, dims_tn, preferred_element_type=f32))
        att_ref[c] = att.astype(bf16)
        prob_grad = lax.dot_general(v, da_rows, dims_nt, preferred_element_type=f32)
        score_grad = (
            prob * (prob_grad - jnp.sum(prob * prob_grad, axis=0, keepdims=True)) * scale
        ).astype(bf16)
        d_q = unstack(lax.dot_general(score_grad, k, dims_tn, preferred_element_type=f32))
        d_q = d_q.astype(bf16).astype(f32)
        d_k = jnp.zeros((agents, channels), f32)
        d_v = jnp.zeros((agents, channels), f32)
        zero = jnp.zeros((), bf16)
        for n in range(blocks):
            in_block = row_block == n
            d_k = d_k + jnp.dot(
                jnp.where(in_block, score_grad, zero), q_rows, preferred_element_type=f32
            ).astype(bf16).astype(f32)
            d_v = d_v + jnp.dot(
                jnp.where(in_block, prob_low, zero), da_rows, preferred_element_type=f32
            ).astype(bf16).astype(f32)
        for i, d in enumerate((d_q, d_k, d_v)):
            hi = d.astype(bf16)
            split_ref[0, c, :, i * channels : (i + 1) * channels] = hi
            split_ref[1, c, :, i * channels : (i + 1) * channels] = (d - hi.astype(f32)).astype(bf16)
        return carry

    lax.fori_loop(0, cells, one_cell, 0)


def cell_attention(valid_row, qkv, d_attended, block_size):
    cells, agents, channels = d_attended.shape
    step = 4 if cells % 4 == 0 else 1
    return pl.pallas_call(
        functools.partial(attention_kernel, block_size),
        grid=(cells // step,),
        in_specs=[
            pl.BlockSpec((agents, 1), lambda i: (0, 0)),
            pl.BlockSpec((step, agents, 3 * channels), lambda i: (i, 0, 0)),
            pl.BlockSpec((step, agents, channels), lambda i: (i, 0, 0)),
        ],
        out_specs=[
            pl.BlockSpec((step, agents, channels), lambda i: (i, 0, 0)),
            pl.BlockSpec((2, step, agents, 3 * channels), lambda i: (0, i, 0, 0)),
        ],
        out_shape=[
            jax.ShapeDtypeStruct((cells, agents, channels), jnp.bfloat16),
            jax.ShapeDtypeStruct((2, cells, agents, 3 * channels), jnp.bfloat16),
        ],
        cost_estimate=pl.CostEstimate(
            flops=cells * 48 * agents * HEADS * agents * channels,
            transcendentals=cells * agents * HEADS * agents,
            bytes_accessed=cells * agents * channels * 2 * 11,
        ),
    )(valid_row, qkv, d_attended)


def body(feats, types, valid, offsets, w_qkv, w_out, d_out):
    f32 = jnp.float32
    bf16 = jnp.bfloat16
    highest = lax.Precision.HIGHEST
    own_count, row_count, col_count, channels = feats.shape
    agents = own_count * lax.axis_size("agent")
    first_agent = lax.axis_index("agent") * own_count
    own_offsets = lax.dynamic_slice_in_dim(offsets, first_agent, own_count, 0)
    rimmed = with_halo(feats, (("tile", 1),), MAXOFF)
    warped = relocate(rimmed, own_offsets, 1)
    cell_count = row_count * col_count
    head_size = channels // HEADS
    score_scale = head_size ** (-0.5)
    all_hot = (types[:, None] == jnp.arange(2)[None, :]).astype(bf16)
    flat_feats = warped.reshape(own_count, cell_count, channels)
    flat_grads = d_out.reshape(own_count, cell_count, channels)
    both = lax.all_to_all(
        jnp.concatenate([flat_feats, flat_grads], axis=-1),
        "agent",
        split_axis=1,
        concat_axis=0,
        tiled=True,
    )
    all_feats, all_grads = both[..., :channels], both[..., channels:]
    part_cells = all_feats.shape[1]
    pairs = agents * part_cells
    is_type1 = (types == 1)[None, :, None]
    type_mask = jnp.stack([types == 0, types == 1], axis=0)[:, None, :, None]
    feats_cm = jnp.transpose(all_feats, (1, 0, 2))
    grads_cm = jnp.transpose(all_grads, (1, 0, 2))
    qkv_both = jnp.einsum(
        "gac,tce->tgae", feats_cm, w_qkv, preferred_element_type=f32
    ).astype(bf16)
    qkv = jnp.where(is_type1, qkv_both[1], qkv_both[0])
    d_att_both = jnp.einsum(
        "gae,tce->tgac", grads_cm, w_out, preferred_element_type=f32
    ).astype(bf16)
    d_attended = jnp.where(is_type1, d_att_both[1], d_att_both[0])
    valid_row = (valid == 1).astype(f32).reshape(agents, 1)
    attended, d_split = cell_attention(valid_row, qkv, d_attended, own_count)
    attended_typed = jnp.where(type_mask, attended[None], jnp.zeros((), bf16))
    raw_out = jnp.einsum(
        "tgac,gae->tce", attended_typed, grads_cm, preferred_element_type=f32
    )
    d_part_terms = jnp.einsum(
        "sgae,tce->stgac", d_split, w_qkv, preferred_element_type=f32
    )
    d_part_sum = d_part_terms[0] + d_part_terms[1]
    d_part = jnp.where(is_type1, d_part_sum[1], d_part_sum[0]).astype(bf16)
    d_part = jnp.transpose(d_part, (1, 0, 2))
    returned = lax.all_to_all(d_part, "agent", split_axis=0, concat_axis=1, tiled=True)
    d_warped = returned.reshape(own_count, row_count, col_count, channels)
    feats_typed = jnp.where(type_mask, feats_cm[None], jnp.zeros((), bf16))
    qkv_terms = jnp.einsum(
        "tgac,sgae->stce", feats_typed, d_split, preferred_element_type=f32
    )
    raw_qkv = qkv_terms[0] + qkv_terms[1]
    rimmed_grad = with_halo(d_warped, (("tile", 1),), MAXOFF)
    d_feats = relocate(rimmed_grad, own_offsets, -1)
    norm_limit = math.sqrt(8.0 * channels * channels)
    raw_all = jnp.concatenate([raw_qkv, raw_out], axis=-1)
    tiles = lax.axis_size("tile")
    share_rows = channels // tiles
    pieces = raw_all.reshape(2, tiles, share_rows, 4 * channels).transpose(1, 0, 2, 3)
    share_all = halving_sum(pieces, "tile", tile_bit_order(tiles))
    share_all = doubling_sum(share_all, "agent", list(range(axis_bits("agent"))))
    square_sum = jnp.broadcast_to(jnp.sum(share_all * share_all), (8, 128))
    square_sum = doubling_sum(square_sum, "tile", list(range(axis_bits("tile"))))[0, 0]
    factor = norm_limit / jnp.maximum(jnp.sqrt(square_sum), norm_limit)
    scaled = share_all * factor
    return (d_feats, scaled[..., : 3 * channels], scaled[..., 3 * channels :])


def solution(mesh):
    placed = (
        P("agent", "tile", None, None),
        P(),
        P(),
        P(),
        P(),
        P(),
        P("agent", "tile", None, None),
    )
    return jax.shard_map(
        body,
        mesh=mesh,
        in_specs=placed,
        out_specs=(P("agent", "tile", None, None), P(None, "tile", None), P(None, "tile", None)),
        check_vma=False,
    )
```

```python
import functools
import math

import jax
import jax.numpy as jnp
from jax import lax
from jax.experimental import pallas as pl
from jax.sharding import PartitionSpec as P

HEADS = 8
MAXOFF = 2


def axis_bits(axis):
    count = lax.axis_size(axis)
    bits = count.bit_length() - 1
    assert 1 << bits == count
    return bits


def xor_pairs(count, bit):
    return [(i, i ^ (1 << bit)) for i in range(count)]


def tile_bit_order(count):
    bits = count.bit_length() - 1
    preferred = [0, 1, 4, 2, 5, 3]
    return [b for b in preferred if b < bits] + [b for b in range(bits) if b not in preferred]


def tile_twins(count):
    bits = count.bit_length() - 1
    pairs = {1: 4, 4: 1, 2: 5, 5: 2}
    return {b: t for b, t in pairs.items() if b < bits and t < bits}


def halving_sum(pieces, axis, bit_order, twins):
    count = lax.axis_size(axis)
    me = lax.axis_index(axis)
    bits = axis_bits(axis)
    rest = pieces.shape[1:]
    odd = (me & 1) == 1
    x = pieces.reshape((2,) * bits + rest)
    for step, bit in enumerate(bit_order):
        if step == 1 and twins:
            order = list(range(x.ndim))
            for b, t in twins.items():
                order[bits - 1 - b] = bits - 1 - t
            x = jnp.where(odd, jnp.transpose(x, order), x)
        twin = twins.get(bit, bit) if step > 0 else bit
        dim = bits - 1 - bit
        mine = jnp.where(odd, (me >> twin) & 1, (me >> bit) & 1)
        low = lax.index_in_dim(x, 0, dim, keepdims=True)
        high = lax.index_in_dim(x, 1, dim, keepdims=True)
        keep = jnp.where(mine == 1, high, low)
        send = jnp.where(mine == 1, low, high)
        pairs = [(i, i ^ (1 << (twin if i & 1 else bit))) for i in range(count)]
        x = keep + lax.ppermute(send, axis, pairs)
    return x.reshape(rest)


def doubling_sum(x, axis, bit_order):
    count = lax.axis_size(axis)
    for bit in bit_order:
        x = x + lax.ppermute(x, axis, xor_pairs(count, bit))
    return x


def with_halo(cells, sides, width):
    for axis, dim in sides:
        count = lax.axis_size(axis)
        ends = count - 1
        head = lax.slice_in_dim(cells, 0, width, axis=dim)
        tail = lax.slice_in_dim(cells, cells.shape[dim] - width, cells.shape[dim], axis=dim)
        cells = jnp.concatenate(
            [
                lax.ppermute(tail, axis, [(i, (i + 1) % count) for i in range(ends)]),
                cells,
                lax.ppermute(head, axis, [((i + 1) % count, i) for i in range(ends)]),
            ],
            axis=dim,
        )
    return cells


def relocate(rimmed, offsets, direction):
    padded = jnp.pad(rimmed, ((0, 0), (0, 0), (MAXOFF, MAXOFF), (0, 0)))
    row_count = rimmed.shape[1] - 2 * MAXOFF
    col_count = rimmed.shape[2]

    def pick_one(plane, offset):
        row_start = MAXOFF + direction * offset[0]
        col_start = MAXOFF + direction * offset[1]
        return lax.dynamic_slice(
            plane, (row_start, col_start, jnp.int32(0)), (row_count, col_count, plane.shape[2])
        )

    return jax.vmap(pick_one)(padded, offsets)


def attention_kernel(block_size, valid_ref, qkv_ref, da_ref, att_ref, split_ref):
    f32 = jnp.float32
    bf16 = jnp.bfloat16
    cells, agents, channels = da_ref.shape
    head_size = channels // HEADS
    blocks = agents // block_size
    rows = blocks * HEADS * block_size
    scale = head_size ** (-0.5)
    dims_nt = (((1,), (1,)), ((), ()))
    dims_tn = (((0,), (0,)), ((), ()))
    lane = lax.broadcasted_iota(jnp.int32, (HEADS, channels), 1)
    head = lax.broadcasted_iota(jnp.int32, (HEADS, channels), 0)
    head_mask = (lane // head_size == head).astype(f32).reshape(1, HEADS, 1, channels)
    row_id = lax.broadcasted_iota(jnp.int32, (rows, agents), 0)
    col_id = lax.broadcasted_iota(jnp.int32, (rows, agents), 1)
    row_agent = (row_id // (HEADS * block_size)) * block_size + row_id % block_size
    allowed = (valid_ref[...] > 0.5) | (row_agent == col_id)

    def stack(x):
        spread = x.astype(f32).reshape(blocks, 1, block_size, channels) * head_mask
        return spread.reshape(rows, channels).astype(bf16)

    def unstack(y):
        return jnp.sum(y.reshape(blocks, HEADS, block_size, channels) * head_mask, axis=1).reshape(
            agents, channels
        )

    def one_cell(c, carry):
        q = qkv_ref[c, :, 0:channels]
        k = qkv_ref[c, :, channels : 2 * channels]
        v = qkv_ref[c, :, 2 * channels : 3 * channels]
        q_rows = stack(q)
        da_rows = stack(da_ref[c])
        scores = lax.dot_general(q_rows, k, dims_nt, preferred_element_type=f32) * scale
        raised = jnp.where(allowed, jnp.exp(scores), f32(0.0))
        prob = raised / jnp.sum(raised, axis=1, keepdims=True)
        prob_low = prob.astype(bf16)
        att = unstack(jnp.dot(prob_low, v, preferred_element_type=f32))
        att_ref[c] = att.astype(bf16)
        prob_grad = lax.dot_general(da_rows, v, dims_nt, preferred_element_type=f32)
        score_grad = (
            prob * (prob_grad - jnp.sum(prob * prob_grad, axis=1, keepdims=True)) * scale
        ).astype(bf16)
        d_q = unstack(jnp.dot(score_grad, k, preferred_element_type=f32)).astype(bf16).astype(f32)
        d_k = jnp.zeros((agents, channels), f32)
        d_v = jnp.zeros((agents, channels), f32)
        for n in range(blocks):
            part = slice(n * HEADS * block_size, (n + 1) * HEADS * block_size)
            d_k = d_k + lax.dot_general(
                score_grad[part], q_rows[part], dims_tn, preferred_element_type=f32
            ).astype(bf16).astype(f32)
            d_v = d_v + lax.dot_general(
                prob_low[part], da_rows[part], dims_tn, preferred_element_type=f32
            ).astype(bf16).astype(f32)
        for i, d in enumerate((d_q, d_k, d_v)):
            hi = d.astype(bf16)
            split_ref[0, c, :, i * channels : (i + 1) * channels] = hi
            split_ref[1, c, :, i * channels : (i + 1) * channels] = (d - hi.astype(f32)).astype(bf16)
        return carry

    lax.fori_loop(0, cells, one_cell, 0)


def cell_attention(valid_row, qkv, d_attended, block_size):
    cells, agents, channels = d_attended.shape
    step = 4 if cells % 4 == 0 else 1
    return pl.pallas_call(
        functools.partial(attention_kernel, block_size),
        grid=(cells // step,),
        in_specs=[
            pl.BlockSpec((1, agents), lambda i: (0, 0)),
            pl.BlockSpec((step, agents, 3 * channels), lambda i: (i, 0, 0)),
            pl.BlockSpec((step, agents, channels), lambda i: (i, 0, 0)),
        ],
        out_specs=[
            pl.BlockSpec((step, agents, channels), lambda i: (i, 0, 0)),
            pl.BlockSpec((2, step, agents, 3 * channels), lambda i: (0, i, 0, 0)),
        ],
        out_shape=[
            jax.ShapeDtypeStruct((cells, agents, channels), jnp.bfloat16),
            jax.ShapeDtypeStruct((2, cells, agents, 3 * channels), jnp.bfloat16),
        ],
        cost_estimate=pl.CostEstimate(
            flops=cells * 48 * agents * HEADS * agents * channels,
            transcendentals=cells * agents * HEADS * agents,
            bytes_accessed=cells * agents * channels * 2 * 11,
        ),
    )(valid_row, qkv, d_attended)


def body(feats, types, valid, offsets, w_qkv, w_out, d_out):
    f32 = jnp.float32
    bf16 = jnp.bfloat16
    highest = lax.Precision.HIGHEST
    own_count, row_count, col_count, channels = feats.shape
    agents = own_count * lax.axis_size("agent")
    first_agent = lax.axis_index("agent") * own_count
    own_offsets = lax.dynamic_slice_in_dim(offsets, first_agent, own_count, 0)
    rimmed = with_halo(feats, (("tile", 1),), MAXOFF)
    warped = relocate(rimmed, own_offsets, 1)
    cell_count = row_count * col_count
    head_size = channels // HEADS
    score_scale = head_size ** (-0.5)
    all_hot = (types[:, None] == jnp.arange(2)[None, :]).astype(bf16)
    flat_feats = warped.reshape(own_count, cell_count, channels)
    flat_grads = d_out.reshape(own_count, cell_count, channels)
    both = lax.all_to_all(
        jnp.concatenate([flat_feats, flat_grads], axis=-1),
        "agent",
        split_axis=1,
        concat_axis=0,
        tiled=True,
    )
    all_feats, all_grads = both[..., :channels], both[..., channels:]
    part_cells = all_feats.shape[1]
    pairs = agents * part_cells
    is_type1 = (types == 1)[None, :, None]
    type_mask = jnp.stack([types == 0, types == 1], axis=0)[:, None, :, None]
    feats_cm = jnp.transpose(all_feats, (1, 0, 2))
    grads_cm = jnp.transpose(all_grads, (1, 0, 2))
    qkv_both = jnp.einsum(
        "gac,tce->tgae", feats_cm, w_qkv, preferred_element_type=f32
    ).astype(bf16)
    qkv = jnp.where(is_type1, qkv_both[1], qkv_both[0])
    d_att_both = jnp.einsum(
        "gae,tce->tgac", grads_cm, w_out, preferred_element_type=f32
    ).astype(bf16)
    d_attended = jnp.where(is_type1, d_att_both[1], d_att_both[0])
    valid_row = (valid == 1).astype(f32).reshape(1, agents)
    attended, d_split = cell_attention(valid_row, qkv, d_attended, own_count)
    attended_typed = jnp.where(type_mask, attended[None], jnp.zeros((), bf16))
    raw_out = jnp.einsum(
        "tgac,gae->tce", attended_typed, grads_cm, preferred_element_type=f32
    )
    d_part_terms = jnp.einsum(
        "sgae,tce->stgac", d_split, w_qkv, preferred_element_type=f32
    )
    d_part_sum = d_part_terms[0] + d_part_terms[1]
    d_part = jnp.where(is_type1, d_part_sum[1], d_part_sum[0]).astype(bf16)
    d_part = jnp.transpose(d_part, (1, 0, 2))
    returned = lax.all_to_all(d_part, "agent", split_axis=0, concat_axis=1, tiled=True)
    d_warped = returned.reshape(own_count, row_count, col_count, channels)
    feats_typed = jnp.where(type_mask, feats_cm[None], jnp.zeros((), bf16))
    qkv_terms = jnp.einsum(
        "tgac,sgae->stce", feats_typed, d_split, preferred_element_type=f32
    )
    raw_qkv = qkv_terms[0] + qkv_terms[1]
    rimmed_grad = with_halo(d_warped, (("tile", 1),), MAXOFF)
    d_feats = relocate(rimmed_grad, own_offsets, -1)
    norm_limit = math.sqrt(8.0 * channels * channels)
    raw_all = jnp.concatenate([raw_qkv, raw_out], axis=-1)
    tiles = lax.axis_size("tile")
    share_rows = channels // tiles
    pieces = raw_all.reshape(2, tiles, share_rows, 4 * channels).transpose(1, 0, 2, 3)
    share_all = halving_sum(pieces, "tile", tile_bit_order(tiles), tile_twins(tiles))
    share_all = doubling_sum(share_all, "agent", list(range(axis_bits("agent"))))
    square_sum = jnp.broadcast_to(jnp.sum(share_all * share_all), (8, 128))
    square_sum = doubling_sum(square_sum, "tile", list(range(axis_bits("tile"))))[0, 0]
    factor = norm_limit / jnp.maximum(jnp.sqrt(square_sum), norm_limit)
    scaled = share_all * factor
    return (d_feats, scaled[..., : 3 * channels], scaled[..., 3 * channels :])


def solution(mesh):
    placed = (
        P("agent", "tile", None, None),
        P(),
        P(),
        P(),
        P(),
        P(),
        P("agent", "tile", None, None),
    )
    return jax.shard_map(
        body,
        mesh=mesh,
        in_specs=placed,
        out_specs=(P("agent", "tile", None, None), P(None, "tile", None), P(None, "tile", None)),
        check_vma=False,
    )
```

```python
import functools
import math

import jax
import jax.numpy as jnp
from jax import lax
from jax.experimental import pallas as pl
from jax.sharding import PartitionSpec as P

HEADS = 8
MAXOFF = 2


def axis_bits(axis):
    count = lax.axis_size(axis)
    bits = count.bit_length() - 1
    assert 1 << bits == count
    return bits


def xor_pairs(count, bit):
    return [(i, i ^ (1 << bit)) for i in range(count)]


def tile_bit_order(count):
    bits = count.bit_length() - 1
    preferred = [0, 1, 4, 2, 5, 3]
    return [b for b in preferred if b < bits] + [b for b in range(bits) if b not in preferred]


def tile_twins(count):
    bits = count.bit_length() - 1
    pairs = {1: 4, 4: 1, 2: 5, 5: 2}
    return {b: t for b, t in pairs.items() if b < bits and t < bits}


def halving_sum(pieces, axis, bit_order, twins):
    count = lax.axis_size(axis)
    me = lax.axis_index(axis)
    bits = axis_bits(axis)
    rest = pieces.shape[1:]
    odd = (me & 1) == 1
    x = pieces.reshape((2,) * bits + rest)
    for step, bit in enumerate(bit_order):
        if step == 1 and twins:
            order = list(range(x.ndim))
            for b, t in twins.items():
                order[bits - 1 - b] = bits - 1 - t
            x = jnp.where(odd, jnp.transpose(x, order), x)
        twin = twins.get(bit, bit) if step > 0 else bit
        dim = bits - 1 - bit
        mine = jnp.where(odd, (me >> twin) & 1, (me >> bit) & 1)
        low = lax.index_in_dim(x, 0, dim, keepdims=True)
        high = lax.index_in_dim(x, 1, dim, keepdims=True)
        keep = jnp.where(mine == 1, high, low)
        send = jnp.where(mine == 1, low, high)
        pairs = [(i, i ^ (1 << (twin if i & 1 else bit))) for i in range(count)]
        x = keep + lax.ppermute(send, axis, pairs)
    return x.reshape(rest)


def gather_sum(x, axis):
    count = lax.axis_size(axis)
    copies = jnp.broadcast_to(x[None], (count,) + x.shape)
    held = lax.all_to_all(copies, axis, 0, 0, tiled=True)
    total = held[0]
    for i in range(1, count):
        total = total + held[i]
    return total


def doubling_sum(x, axis, bit_order):
    count = lax.axis_size(axis)
    for bit in bit_order:
        x = x + lax.ppermute(x, axis, xor_pairs(count, bit))
    return x


def with_halo(cells, sides, width):
    for axis, dim in sides:
        count = lax.axis_size(axis)
        ends = count - 1
        head = lax.slice_in_dim(cells, 0, width, axis=dim)
        tail = lax.slice_in_dim(cells, cells.shape[dim] - width, cells.shape[dim], axis=dim)
        cells = jnp.concatenate(
            [
                lax.ppermute(tail, axis, [(i, (i + 1) % count) for i in range(ends)]),
                cells,
                lax.ppermute(head, axis, [((i + 1) % count, i) for i in range(ends)]),
            ],
            axis=dim,
        )
    return cells


def relocate(rimmed, offsets, direction):
    padded = jnp.pad(rimmed, ((0, 0), (0, 0), (MAXOFF, MAXOFF), (0, 0)))
    row_count = rimmed.shape[1] - 2 * MAXOFF
    col_count = rimmed.shape[2]

    def pick_one(plane, offset):
        row_start = MAXOFF + direction * offset[0]
        col_start = MAXOFF + direction * offset[1]
        return lax.dynamic_slice(
            plane, (row_start, col_start, jnp.int32(0)), (row_count, col_count, plane.shape[2])
        )

    return jax.vmap(pick_one)(padded, offsets)


def attention_kernel(block_size, valid_ref, qkv_ref, da_ref, att_ref, split_ref):
    f32 = jnp.float32
    bf16 = jnp.bfloat16
    cells, agents, channels = da_ref.shape
    head_size = channels // HEADS
    blocks = agents // block_size
    rows = blocks * HEADS * block_size
    scale = head_size ** (-0.5)
    dims_nt = (((1,), (1,)), ((), ()))
    dims_tn = (((0,), (0,)), ((), ()))
    lane = lax.broadcasted_iota(jnp.int32, (HEADS, channels), 1)
    head = lax.broadcasted_iota(jnp.int32, (HEADS, channels), 0)
    head_mask = (lane // head_size == head).astype(f32).reshape(1, HEADS, 1, channels)
    row_id = lax.broadcasted_iota(jnp.int32, (rows, agents), 0)
    col_id = lax.broadcasted_iota(jnp.int32, (rows, agents), 1)
    row_agent = (row_id // (HEADS * block_size)) * block_size + row_id % block_size
    allowed = (valid_ref[...] > 0.5) | (row_agent == col_id)

    def stack(x):
        spread = x.astype(f32).reshape(blocks, 1, block_size, channels) * head_mask
        return spread.reshape(rows, channels).astype(bf16)

    def unstack(y):
        return jnp.sum(y.reshape(blocks, HEADS, block_size, channels) * head_mask, axis=1).reshape(
            agents, channels
        )

    def one_cell(c, carry):
        q = qkv_ref[c, :, 0:channels]
        k = qkv_ref[c, :, channels : 2 * channels]
        v = qkv_ref[c, :, 2 * channels : 3 * channels]
        q_rows = stack(q)
        da_rows = stack(da_ref[c])
        scores = lax.dot_general(q_rows, k, dims_nt, preferred_element_type=f32) * scale
        raised = jnp.where(allowed, jnp.exp(scores), f32(0.0))
        prob = raised / jnp.sum(raised, axis=1, keepdims=True)
        prob_low = prob.astype(bf16)
        att = unstack(jnp.dot(prob_low, v, preferred_element_type=f32))
        att_ref[c] = att.astype(bf16)
        prob_grad = lax.dot_general(da_rows, v, dims_nt, preferred_element_type=f32)
        score_grad = (
            prob * (prob_grad - jnp.sum(prob * prob_grad, axis=1, keepdims=True)) * scale
        ).astype(bf16)
        d_q = unstack(jnp.dot(score_grad, k, preferred_element_type=f32)).astype(bf16).astype(f32)
        d_k = jnp.zeros((agents, channels), f32)
        d_v = jnp.zeros((agents, channels), f32)
        for n in range(blocks):
            part = slice(n * HEADS * block_size, (n + 1) * HEADS * block_size)
            d_k = d_k + lax.dot_general(
                score_grad[part], q_rows[part], dims_tn, preferred_element_type=f32
            ).astype(bf16).astype(f32)
            d_v = d_v + lax.dot_general(
                prob_low[part], da_rows[part], dims_tn, preferred_element_type=f32
            ).astype(bf16).astype(f32)
        for i, d in enumerate((d_q, d_k, d_v)):
            hi = d.astype(bf16)
            split_ref[0, c, :, i * channels : (i + 1) * channels] = hi
            split_ref[1, c, :, i * channels : (i + 1) * channels] = (d - hi.astype(f32)).astype(bf16)
        return carry

    lax.fori_loop(0, cells, one_cell, 0)


def cell_attention(valid_row, qkv, d_attended, block_size):
    cells, agents, channels = d_attended.shape
    step = 4 if cells % 4 == 0 else 1
    return pl.pallas_call(
        functools.partial(attention_kernel, block_size),
        grid=(cells // step,),
        in_specs=[
            pl.BlockSpec((1, agents), lambda i: (0, 0)),
            pl.BlockSpec((step, agents, 3 * channels), lambda i: (i, 0, 0)),
            pl.BlockSpec((step, agents, channels), lambda i: (i, 0, 0)),
        ],
        out_specs=[
            pl.BlockSpec((step, agents, channels), lambda i: (i, 0, 0)),
            pl.BlockSpec((2, step, agents, 3 * channels), lambda i: (0, i, 0, 0)),
        ],
        out_shape=[
            jax.ShapeDtypeStruct((cells, agents, channels), jnp.bfloat16),
            jax.ShapeDtypeStruct((2, cells, agents, 3 * channels), jnp.bfloat16),
        ],
        cost_estimate=pl.CostEstimate(
            flops=cells * 48 * agents * HEADS * agents * channels,
            transcendentals=cells * agents * HEADS * agents,
            bytes_accessed=cells * agents * channels * 2 * 11,
        ),
    )(valid_row, qkv, d_attended)


def body(feats, types, valid, offsets, w_qkv, w_out, d_out):
    f32 = jnp.float32
    bf16 = jnp.bfloat16
    highest = lax.Precision.HIGHEST
    own_count, row_count, col_count, channels = feats.shape
    agents = own_count * lax.axis_size("agent")
    first_agent = lax.axis_index("agent") * own_count
    own_offsets = lax.dynamic_slice_in_dim(offsets, first_agent, own_count, 0)
    rimmed = with_halo(feats, (("tile", 1),), MAXOFF)
    warped = relocate(rimmed, own_offsets, 1)
    cell_count = row_count * col_count
    head_size = channels // HEADS
    score_scale = head_size ** (-0.5)
    all_hot = (types[:, None] == jnp.arange(2)[None, :]).astype(bf16)
    flat_feats = warped.reshape(own_count, cell_count, channels)
    flat_grads = d_out.reshape(own_count, cell_count, channels)
    both = lax.all_to_all(
        jnp.concatenate([flat_feats, flat_grads], axis=-1),
        "agent",
        split_axis=1,
        concat_axis=0,
        tiled=True,
    )
    all_feats, all_grads = both[..., :channels], both[..., channels:]
    part_cells = all_feats.shape[1]
    pairs = agents * part_cells
    is_type1 = (types == 1)[None, :, None]
    type_mask = jnp.stack([types == 0, types == 1], axis=0)[:, None, :, None]
    feats_cm = jnp.transpose(all_feats, (1, 0, 2))
    grads_cm = jnp.transpose(all_grads, (1, 0, 2))
    qkv_both = jnp.einsum(
        "gac,tce->tgae", feats_cm, w_qkv, preferred_element_type=f32
    ).astype(bf16)
    qkv = jnp.where(is_type1, qkv_both[1], qkv_both[0])
    d_att_both = jnp.einsum(
        "gae,tce->tgac", grads_cm, w_out, preferred_element_type=f32
    ).astype(bf16)
    d_attended = jnp.where(is_type1, d_att_both[1], d_att_both[0])
    valid_row = (valid == 1).astype(f32).reshape(1, agents)
    attended, d_split = cell_attention(valid_row, qkv, d_attended, own_count)
    attended_typed = jnp.where(type_mask, attended[None], jnp.zeros((), bf16))
    raw_out = jnp.einsum(
        "tgac,gae->tce", attended_typed, grads_cm, preferred_element_type=f32
    )
    d_part_terms = jnp.einsum(
        "sgae,tce->stgac", d_split, w_qkv, preferred_element_type=f32
    )
    d_part_sum = d_part_terms[0] + d_part_terms[1]
    d_part = jnp.where(is_type1, d_part_sum[1], d_part_sum[0]).astype(bf16)
    d_part = jnp.transpose(d_part, (1, 0, 2))
    returned = lax.all_to_all(d_part, "agent", split_axis=0, concat_axis=1, tiled=True)
    d_warped = returned.reshape(own_count, row_count, col_count, channels)
    feats_typed = jnp.where(type_mask, feats_cm[None], jnp.zeros((), bf16))
    qkv_terms = jnp.einsum(
        "tgac,sgae->stce", feats_typed, d_split, preferred_element_type=f32
    )
    raw_qkv = qkv_terms[0] + qkv_terms[1]
    rimmed_grad = with_halo(d_warped, (("tile", 1),), MAXOFF)
    d_feats = relocate(rimmed_grad, own_offsets, -1)
    norm_limit = math.sqrt(8.0 * channels * channels)
    raw_all = jnp.concatenate([raw_qkv, raw_out], axis=-1)
    tiles = lax.axis_size("tile")
    share_rows = channels // tiles
    pieces = raw_all.reshape(2, tiles, share_rows, 4 * channels).transpose(1, 0, 2, 3)
    share_all = halving_sum(pieces, "tile", tile_bit_order(tiles), tile_twins(tiles))
    share_all = gather_sum(share_all, "agent")
    square_sum = jnp.sum(share_all * share_all).reshape(1, 1)
    square_sum = gather_sum(jnp.broadcast_to(square_sum, (1, 128)), "tile")[0, 0]
    factor = norm_limit / jnp.maximum(jnp.sqrt(square_sum), norm_limit)
    scaled = share_all * factor
    return (d_feats, scaled[..., : 3 * channels], scaled[..., 3 * channels :])


def solution(mesh):
    placed = (
        P("agent", "tile", None, None),
        P(),
        P(),
        P(),
        P(),
        P(),
        P("agent", "tile", None, None),
    )
    return jax.shard_map(
        body,
        mesh=mesh,
        in_specs=placed,
        out_specs=(P("agent", "tile", None, None), P(None, "tile", None), P(None, "tile", None)),
        check_vma=False,
    )
```

```python
import functools
import math

import jax
import jax.numpy as jnp
from jax import lax
from jax.experimental import pallas as pl
from jax.sharding import PartitionSpec as P

HEADS = 8
MAXOFF = 2


def axis_bits(axis):
    count = lax.axis_size(axis)
    bits = count.bit_length() - 1
    assert 1 << bits == count
    return bits


def xor_pairs(count, bit):
    return [(i, i ^ (1 << bit)) for i in range(count)]


def tile_bit_order(count):
    bits = count.bit_length() - 1
    preferred = [0, 1, 4, 2, 5, 3]
    return [b for b in preferred if b < bits] + [b for b in range(bits) if b not in preferred]


def tile_twins(count):
    bits = count.bit_length() - 1
    pairs = {1: 4, 4: 1, 2: 5, 5: 2}
    return {b: t for b, t in pairs.items() if b < bits and t < bits}


def halving_sum(pieces, axis, bit_order, twins):
    count = lax.axis_size(axis)
    me = lax.axis_index(axis)
    bits = axis_bits(axis)
    rest = pieces.shape[1:]
    odd = (me & 1) == 1
    x = pieces.reshape((2,) * bits + rest)
    for step, bit in enumerate(bit_order):
        if step == 1 and twins:
            order = list(range(x.ndim))
            for b, t in twins.items():
                order[bits - 1 - b] = bits - 1 - t
            x = jnp.where(odd, jnp.transpose(x, order), x)
        twin = twins.get(bit, bit) if step > 0 else bit
        dim = bits - 1 - bit
        mine = jnp.where(odd, (me >> twin) & 1, (me >> bit) & 1)
        low = lax.index_in_dim(x, 0, dim, keepdims=True)
        high = lax.index_in_dim(x, 1, dim, keepdims=True)
        keep = jnp.where(mine == 1, high, low)
        send = jnp.where(mine == 1, low, high)
        pairs = [(i, i ^ (1 << (twin if i & 1 else bit))) for i in range(count)]
        x = keep + lax.ppermute(send, axis, pairs)
    return x.reshape(rest)


def gather_sum(x, axis):
    count = lax.axis_size(axis)
    copies = jnp.broadcast_to(x[None], (count,) + x.shape)
    held = lax.all_to_all(copies, axis, 0, 0, tiled=True)
    total = held[0]
    for i in range(1, count):
        total = total + held[i]
    return total


def doubling_sum(x, axis, bit_order):
    count = lax.axis_size(axis)
    for bit in bit_order:
        x = x + lax.ppermute(x, axis, xor_pairs(count, bit))
    return x


def with_halo(cells, sides, width):
    for axis, dim in sides:
        count = lax.axis_size(axis)
        ends = count - 1
        head = lax.slice_in_dim(cells, 0, width, axis=dim)
        tail = lax.slice_in_dim(cells, cells.shape[dim] - width, cells.shape[dim], axis=dim)
        cells = jnp.concatenate(
            [
                lax.ppermute(tail, axis, [(i, (i + 1) % count) for i in range(ends)]),
                cells,
                lax.ppermute(head, axis, [((i + 1) % count, i) for i in range(ends)]),
            ],
            axis=dim,
        )
    return cells


def relocate(rimmed, offsets, direction):
    padded = jnp.pad(rimmed, ((0, 0), (0, 0), (MAXOFF, MAXOFF), (0, 0)))
    row_count = rimmed.shape[1] - 2 * MAXOFF
    col_count = rimmed.shape[2]

    def pick_one(plane, offset):
        row_start = MAXOFF + direction * offset[0]
        col_start = MAXOFF + direction * offset[1]
        return lax.dynamic_slice(
            plane, (row_start, col_start, jnp.int32(0)), (row_count, col_count, plane.shape[2])
        )

    return jax.vmap(pick_one)(padded, offsets)


def attention_kernel(block_size, valid_ref, qkv_ref, da_ref, att_ref, split_ref):
    f32 = jnp.float32
    bf16 = jnp.bfloat16
    cells, agents, channels = da_ref.shape
    head_size = channels // HEADS
    blocks = agents // block_size
    rows = blocks * HEADS * block_size
    scale = head_size ** (-0.5)
    dims_nt = (((1,), (1,)), ((), ()))
    dims_tn = (((0,), (0,)), ((), ()))
    lane = lax.broadcasted_iota(jnp.int32, (HEADS, channels), 1)
    head = lax.broadcasted_iota(jnp.int32, (HEADS, channels), 0)
    head_mask = (lane // head_size == head).astype(f32).reshape(1, HEADS, 1, channels)
    row_id = lax.broadcasted_iota(jnp.int32, (rows, agents), 0)
    col_id = lax.broadcasted_iota(jnp.int32, (rows, agents), 1)
    row_agent = (row_id // (HEADS * block_size)) * block_size + row_id % block_size
    allowed = (valid_ref[...] > 0.5) | (row_agent == col_id)

    def stack(x):
        spread = x.astype(f32).reshape(blocks, 1, block_size, channels) * head_mask
        return spread.reshape(rows, channels).astype(bf16)

    def unstack(y):
        return jnp.sum(y.reshape(blocks, HEADS, block_size, channels) * head_mask, axis=1).reshape(
            agents, channels
        )

    def one_cell(c, carry):
        q = qkv_ref[c, :, 0:channels]
        k = qkv_ref[c, :, channels : 2 * channels]
        v = qkv_ref[c, :, 2 * channels : 3 * channels]
        q_rows = stack(q)
        da_rows = stack(da_ref[c])
        scores = lax.dot_general(q_rows, k, dims_nt, preferred_element_type=f32) * scale
        raised = jnp.where(allowed, jnp.exp(scores), f32(0.0))
        prob = raised / jnp.sum(raised, axis=1, keepdims=True)
        prob_low = prob.astype(bf16)
        att = unstack(jnp.dot(prob_low, v, preferred_element_type=f32))
        att_ref[c] = att.astype(bf16)
        prob_grad = lax.dot_general(da_rows, v, dims_nt, preferred_element_type=f32)
        score_grad = (
            prob * (prob_grad - jnp.sum(prob * prob_grad, axis=1, keepdims=True)) * scale
        ).astype(bf16)
        d_q = unstack(jnp.dot(score_grad, k, preferred_element_type=f32)).astype(bf16).astype(f32)
        d_k = jnp.zeros((agents, channels), f32)
        d_v = jnp.zeros((agents, channels), f32)
        for n in range(blocks):
            part = slice(n * HEADS * block_size, (n + 1) * HEADS * block_size)
            d_k = d_k + lax.dot_general(
                score_grad[part], q_rows[part], dims_tn, preferred_element_type=f32
            ).astype(bf16).astype(f32)
            d_v = d_v + lax.dot_general(
                prob_low[part], da_rows[part], dims_tn, preferred_element_type=f32
            ).astype(bf16).astype(f32)
        for i, d in enumerate((d_q, d_k, d_v)):
            hi = d.astype(bf16)
            split_ref[0, c, :, i * channels : (i + 1) * channels] = hi
            split_ref[1, c, :, i * channels : (i + 1) * channels] = (d - hi.astype(f32)).astype(bf16)
        return carry

    lax.fori_loop(0, cells, one_cell, 0)


def cell_attention(valid_row, qkv, d_attended, block_size):
    cells, agents, channels = d_attended.shape
    step = 4 if cells % 4 == 0 else 1
    return pl.pallas_call(
        functools.partial(attention_kernel, block_size),
        grid=(cells // step,),
        in_specs=[
            pl.BlockSpec((1, agents), lambda i: (0, 0)),
            pl.BlockSpec((step, agents, 3 * channels), lambda i: (i, 0, 0)),
            pl.BlockSpec((step, agents, channels), lambda i: (i, 0, 0)),
        ],
        out_specs=[
            pl.BlockSpec((step, agents, channels), lambda i: (i, 0, 0)),
            pl.BlockSpec((2, step, agents, 3 * channels), lambda i: (0, i, 0, 0)),
        ],
        out_shape=[
            jax.ShapeDtypeStruct((cells, agents, channels), jnp.bfloat16),
            jax.ShapeDtypeStruct((2, cells, agents, 3 * channels), jnp.bfloat16),
        ],
        cost_estimate=pl.CostEstimate(
            flops=cells * 48 * agents * HEADS * agents * channels,
            transcendentals=cells * agents * HEADS * agents,
            bytes_accessed=cells * agents * channels * 2 * 11,
        ),
    )(valid_row, qkv, d_attended)


def body(feats, types, valid, offsets, w_qkv, w_out, d_out):
    f32 = jnp.float32
    bf16 = jnp.bfloat16
    highest = lax.Precision.HIGHEST
    own_count, row_count, col_count, channels = feats.shape
    agents = own_count * lax.axis_size("agent")
    first_agent = lax.axis_index("agent") * own_count
    own_offsets = lax.dynamic_slice_in_dim(offsets, first_agent, own_count, 0)
    rimmed = with_halo(feats, (("tile", 1),), MAXOFF)
    warped = relocate(rimmed, own_offsets, 1)
    cell_count = row_count * col_count
    head_size = channels // HEADS
    score_scale = head_size ** (-0.5)
    all_hot = (types[:, None] == jnp.arange(2)[None, :]).astype(bf16)
    flat_feats = warped.reshape(own_count, cell_count, channels)
    flat_grads = d_out.reshape(own_count, cell_count, channels)
    both = lax.all_to_all(
        jnp.concatenate([flat_feats, flat_grads], axis=-1),
        "agent",
        split_axis=1,
        concat_axis=0,
        tiled=True,
    )
    all_feats, all_grads = both[..., :channels], both[..., channels:]
    part_cells = all_feats.shape[1]
    pairs = agents * part_cells
    is_type1 = (types == 1)[None, :, None]
    type_mask = jnp.stack([types == 0, types == 1], axis=0)[:, None, :, None]
    feats_cm = jnp.transpose(all_feats, (1, 0, 2))
    grads_cm = jnp.transpose(all_grads, (1, 0, 2))
    qkv_both = jnp.einsum(
        "gac,tce->tgae", feats_cm, w_qkv, preferred_element_type=f32
    ).astype(bf16)
    qkv = jnp.where(is_type1, qkv_both[1], qkv_both[0])
    d_att_both = jnp.einsum(
        "gae,tce->tgac", grads_cm, w_out, preferred_element_type=f32
    ).astype(bf16)
    d_attended = jnp.where(is_type1, d_att_both[1], d_att_both[0])
    valid_row = (valid == 1).astype(f32).reshape(1, agents)
    attended, d_split = cell_attention(valid_row, qkv, d_attended, own_count)
    attended_typed = jnp.where(type_mask, attended[None], jnp.zeros((), bf16))
    raw_out = jnp.einsum(
        "tgac,gae->cte", attended_typed, grads_cm, preferred_element_type=f32
    )
    d_part_terms = jnp.einsum(
        "sgae,tce->stgac", d_split, w_qkv, preferred_element_type=f32
    )
    d_part_sum = d_part_terms[0] + d_part_terms[1]
    d_part = jnp.where(is_type1, d_part_sum[1], d_part_sum[0]).astype(bf16)
    d_part = jnp.transpose(d_part, (1, 0, 2))
    returned = lax.all_to_all(d_part, "agent", split_axis=0, concat_axis=1, tiled=True)
    d_warped = returned.reshape(own_count, row_count, col_count, channels)
    feats_typed = jnp.where(type_mask, feats_cm[None], jnp.zeros((), bf16))
    qkv_terms = jnp.einsum(
        "tgac,sgae->scte", feats_typed, d_split, preferred_element_type=f32
    )
    raw_qkv = qkv_terms[0] + qkv_terms[1]
    rimmed_grad = with_halo(d_warped, (("tile", 1),), MAXOFF)
    d_feats = relocate(rimmed_grad, own_offsets, -1)
    norm_limit = math.sqrt(8.0 * channels * channels)
    raw_all = jnp.concatenate([raw_qkv, raw_out], axis=-1)
    tiles = lax.axis_size("tile")
    share_rows = channels // tiles
    pieces = raw_all.reshape(tiles, share_rows, 2, 4 * channels)
    share_all = halving_sum(pieces, "tile", tile_bit_order(tiles), tile_twins(tiles))
    share_all = gather_sum(share_all, "agent")
    square_sum = jnp.sum(share_all * share_all).reshape(1, 1)
    square_sum = gather_sum(jnp.broadcast_to(square_sum, (1, 128)), "tile")[0, 0]
    factor = norm_limit / jnp.maximum(jnp.sqrt(square_sum), norm_limit)
    scaled = share_all * factor
    scaled = jnp.transpose(scaled, (1, 0, 2))
    return (d_feats, scaled[..., : 3 * channels], scaled[..., 3 * channels :])


def solution(mesh):
    placed = (
        P("agent", "tile", None, None),
        P(),
        P(),
        P(),
        P(),
        P(),
        P("agent", "tile", None, None),
    )
    return jax.shard_map(
        body,
        mesh=mesh,
        in_specs=placed,
        out_specs=(P("agent", "tile", None, None), P(None, "tile", None), P(None, "tile", None)),
        check_vma=False,
    )
```

```python
import functools
import math

import jax
import jax.numpy as jnp
from jax import lax
from jax.experimental import pallas as pl
from jax.sharding import Mesh, PartitionSpec as P

HEADS = 8
TILE = ("x", "z", "core")
MAXOFF = 2


def axis_bits(axis):
    count = lax.axis_size(axis)
    bits = count.bit_length() - 1
    assert 1 << bits == count
    return bits


def xor_pairs(count, bit):
    return [(i, i ^ (1 << bit)) for i in range(count)]


def tile_bit_order(count):
    bits = count.bit_length() - 1
    preferred = [0, 1, 4, 2, 5, 3]
    return [b for b in preferred if b < bits] + [b for b in range(bits) if b not in preferred]


def tile_twins(count):
    bits = count.bit_length() - 1
    pairs = {1: 4, 4: 1, 2: 5, 5: 2}
    return {b: t for b, t in pairs.items() if b < bits and t < bits}


def halving_sum(pieces, axis, bit_order, twins):
    count = lax.axis_size(axis)
    me = lax.axis_index(axis)
    bits = axis_bits(axis)
    rest = pieces.shape[1:]
    odd = (me & 1) == 1
    x = pieces.reshape((2,) * bits + rest)
    for step, bit in enumerate(bit_order):
        if step == 1 and twins:
            order = list(range(x.ndim))
            for b, t in twins.items():
                order[bits - 1 - b] = bits - 1 - t
            x = jnp.where(odd, jnp.transpose(x, order), x)
        twin = twins.get(bit, bit) if step > 0 else bit
        dim = bits - 1 - bit
        mine = jnp.where(odd, (me >> twin) & 1, (me >> bit) & 1)
        low = lax.index_in_dim(x, 0, dim, keepdims=True)
        high = lax.index_in_dim(x, 1, dim, keepdims=True)
        keep = jnp.where(mine == 1, high, low)
        send = jnp.where(mine == 1, low, high)
        pairs = [(i, i ^ (1 << (twin if i & 1 else bit))) for i in range(count)]
        x = keep + lax.ppermute(send, axis, pairs)
    return x.reshape(rest)


def gather_sum(x, axis):
    count = lax.axis_size(axis)
    copies = jnp.broadcast_to(x[None], (count,) + x.shape)
    held = lax.all_to_all(copies, axis, 0, 0, tiled=True)
    total = held[0]
    for i in range(1, count):
        total = total + held[i]
    return total


def doubling_sum(x, axis, bit_order):
    count = lax.axis_size(axis)
    for bit in bit_order:
        x = x + lax.ppermute(x, axis, xor_pairs(count, bit))
    return x


def with_halo(cells, sides, width):
    for axis, dim in sides:
        count = lax.axis_size(axis)
        ends = count - 1
        head = lax.slice_in_dim(cells, 0, width, axis=dim)
        tail = lax.slice_in_dim(cells, cells.shape[dim] - width, cells.shape[dim], axis=dim)
        cells = jnp.concatenate(
            [
                lax.ppermute(tail, axis, [(i, (i + 1) % count) for i in range(ends)]),
                cells,
                lax.ppermute(head, axis, [((i + 1) % count, i) for i in range(ends)]),
            ],
            axis=dim,
        )
    return cells


def relocate(rimmed, offsets, direction):
    padded = jnp.pad(rimmed, ((0, 0), (0, 0), (MAXOFF, MAXOFF), (0, 0)))
    row_count = rimmed.shape[1] - 2 * MAXOFF
    col_count = rimmed.shape[2]

    def pick_one(plane, offset):
        row_start = MAXOFF + direction * offset[0]
        col_start = MAXOFF + direction * offset[1]
        return lax.dynamic_slice(
            plane, (row_start, col_start, jnp.int32(0)), (row_count, col_count, plane.shape[2])
        )

    return jax.vmap(pick_one)(padded, offsets)


def attention_kernel(block_size, valid_ref, qkv_ref, da_ref, att_ref, split_ref):
    f32 = jnp.float32
    bf16 = jnp.bfloat16
    cells, agents, channels = da_ref.shape
    head_size = channels // HEADS
    blocks = agents // block_size
    rows = blocks * HEADS * block_size
    scale = head_size ** (-0.5)
    dims_nt = (((1,), (1,)), ((), ()))
    dims_tn = (((0,), (0,)), ((), ()))
    lane = lax.broadcasted_iota(jnp.int32, (HEADS, channels), 1)
    head = lax.broadcasted_iota(jnp.int32, (HEADS, channels), 0)
    head_mask = (lane // head_size == head).astype(f32).reshape(1, HEADS, 1, channels)
    row_id = lax.broadcasted_iota(jnp.int32, (rows, agents), 0)
    col_id = lax.broadcasted_iota(jnp.int32, (rows, agents), 1)
    row_agent = (row_id // (HEADS * block_size)) * block_size + row_id % block_size
    allowed = (valid_ref[...] > 0.5) | (row_agent == col_id)

    def stack(x):
        spread = x.astype(f32).reshape(blocks, 1, block_size, channels) * head_mask
        return spread.reshape(rows, channels).astype(bf16)

    def unstack(y):
        return jnp.sum(y.reshape(blocks, HEADS, block_size, channels) * head_mask, axis=1).reshape(
            agents, channels
        )

    def one_cell(c, carry):
        q = qkv_ref[c, :, 0:channels]
        k = qkv_ref[c, :, channels : 2 * channels]
        v = qkv_ref[c, :, 2 * channels : 3 * channels]
        q_rows = stack(q)
        da_rows = stack(da_ref[c])
        scores = lax.dot_general(q_rows, k, dims_nt, preferred_element_type=f32) * scale
        raised = jnp.where(allowed, jnp.exp(scores), f32(0.0))
        prob = raised / jnp.sum(raised, axis=1, keepdims=True)
        prob_low = prob.astype(bf16)
        att = unstack(jnp.dot(prob_low, v, preferred_element_type=f32))
        att_ref[c] = att.astype(bf16)
        prob_grad = lax.dot_general(da_rows, v, dims_nt, preferred_element_type=f32)
        score_grad = (
            prob * (prob_grad - jnp.sum(prob * prob_grad, axis=1, keepdims=True)) * scale
        ).astype(bf16)
        d_q = unstack(jnp.dot(score_grad, k, preferred_element_type=f32)).astype(bf16).astype(f32)
        d_k = jnp.zeros((agents, channels), f32)
        d_v = jnp.zeros((agents, channels), f32)
        for n in range(blocks):
            part = slice(n * HEADS * block_size, (n + 1) * HEADS * block_size)
            d_k = d_k + lax.dot_general(
                score_grad[part], q_rows[part], dims_tn, preferred_element_type=f32
            ).astype(bf16).astype(f32)
            d_v = d_v + lax.dot_general(
                prob_low[part], da_rows[part], dims_tn, preferred_element_type=f32
            ).astype(bf16).astype(f32)
        for i, d in enumerate((d_q, d_k, d_v)):
            hi = d.astype(bf16)
            split_ref[0, c, :, i * channels : (i + 1) * channels] = hi
            split_ref[1, c, :, i * channels : (i + 1) * channels] = (d - hi.astype(f32)).astype(bf16)
        return carry

    lax.fori_loop(0, cells, one_cell, 0)


def cell_attention(valid_row, qkv, d_attended, block_size):
    cells, agents, channels = d_attended.shape
    step = 4 if cells % 4 == 0 else 1
    return pl.pallas_call(
        functools.partial(attention_kernel, block_size),
        grid=(cells // step,),
        in_specs=[
            pl.BlockSpec((1, agents), lambda i: (0, 0)),
            pl.BlockSpec((step, agents, 3 * channels), lambda i: (i, 0, 0)),
            pl.BlockSpec((step, agents, channels), lambda i: (i, 0, 0)),
        ],
        out_specs=[
            pl.BlockSpec((step, agents, channels), lambda i: (i, 0, 0)),
            pl.BlockSpec((2, step, agents, 3 * channels), lambda i: (0, i, 0, 0)),
        ],
        out_shape=[
            jax.ShapeDtypeStruct((cells, agents, channels), jnp.bfloat16),
            jax.ShapeDtypeStruct((2, cells, agents, 3 * channels), jnp.bfloat16),
        ],
        cost_estimate=pl.CostEstimate(
            flops=cells * 48 * agents * HEADS * agents * channels,
            transcendentals=cells * agents * HEADS * agents,
            bytes_accessed=cells * agents * channels * 2 * 11,
        ),
    )(valid_row, qkv, d_attended)


def body(feats, types, valid, offsets, w_qkv, w_out, d_out):
    f32 = jnp.float32
    bf16 = jnp.bfloat16
    highest = lax.Precision.HIGHEST
    own_count, row_count, col_count, channels = feats.shape
    agents = own_count * lax.axis_size("agent")
    first_agent = lax.axis_index("agent") * own_count
    own_offsets = lax.dynamic_slice_in_dim(offsets, first_agent, own_count, 0)
    rimmed = with_halo(feats, ((TILE, 1),), MAXOFF)
    warped = relocate(rimmed, own_offsets, 1)
    cell_count = row_count * col_count
    head_size = channels // HEADS
    score_scale = head_size ** (-0.5)
    all_hot = (types[:, None] == jnp.arange(2)[None, :]).astype(bf16)
    flat_feats = warped.reshape(own_count, cell_count, channels)
    flat_grads = d_out.reshape(own_count, cell_count, channels)
    both = lax.all_to_all(
        jnp.concatenate([flat_feats, flat_grads], axis=-1),
        "agent",
        split_axis=1,
        concat_axis=0,
        tiled=True,
    )
    all_feats, all_grads = both[..., :channels], both[..., channels:]
    part_cells = all_feats.shape[1]
    pairs = agents * part_cells
    is_type1 = (types == 1)[None, :, None]
    type_mask = jnp.stack([types == 0, types == 1], axis=0)[:, None, :, None]
    feats_cm = jnp.transpose(all_feats, (1, 0, 2))
    grads_cm = jnp.transpose(all_grads, (1, 0, 2))
    qkv_both = jnp.einsum(
        "gac,tce->tgae", feats_cm, w_qkv, preferred_element_type=f32
    ).astype(bf16)
    qkv = jnp.where(is_type1, qkv_both[1], qkv_both[0])
    d_att_both = jnp.einsum(
        "gae,tce->tgac", grads_cm, w_out, preferred_element_type=f32
    ).astype(bf16)
    d_attended = jnp.where(is_type1, d_att_both[1], d_att_both[0])
    valid_row = (valid == 1).astype(f32).reshape(1, agents)
    attended, d_split = cell_attention(valid_row, qkv, d_attended, own_count)
    attended_typed = jnp.where(type_mask, attended[None], jnp.zeros((), bf16))
    raw_out = jnp.einsum(
        "tgac,gae->cte", attended_typed, grads_cm, preferred_element_type=f32
    )
    d_part_terms = jnp.einsum(
        "sgae,tce->stgac", d_split, w_qkv, preferred_element_type=f32
    )
    d_part_sum = d_part_terms[0] + d_part_terms[1]
    d_part = jnp.where(is_type1, d_part_sum[1], d_part_sum[0]).astype(bf16)
    d_part = jnp.transpose(d_part, (1, 0, 2))
    returned = lax.all_to_all(d_part, "agent", split_axis=0, concat_axis=1, tiled=True)
    d_warped = returned.reshape(own_count, row_count, col_count, channels)
    feats_typed = jnp.where(type_mask, feats_cm[None], jnp.zeros((), bf16))
    qkv_terms = jnp.einsum(
        "tgac,sgae->scte", feats_typed, d_split, preferred_element_type=f32
    )
    raw_qkv = qkv_terms[0] + qkv_terms[1]
    rimmed_grad = with_halo(d_warped, ((TILE, 1),), MAXOFF)
    d_feats = relocate(rimmed_grad, own_offsets, -1)
    norm_limit = math.sqrt(8.0 * channels * channels)
    raw_all = jnp.concatenate([raw_qkv, raw_out], axis=-1)
    sizes = [lax.axis_size(name) for name in TILE]
    share_rows = channels // math.prod(sizes)
    pieces = raw_all.reshape(*sizes, share_rows, 2, 4 * channels)
    core_at = len(sizes) - 1
    mine = lax.axis_index("core")
    keep = lax.dynamic_index_in_dim(pieces, mine, core_at, keepdims=False)
    send = lax.dynamic_index_in_dim(pieces, 1 - mine, core_at, keepdims=False)
    share_all = keep + lax.ppermute(send, "core", [(0, 1), (1, 0)])
    for dim, name in ((0, "x"), (0, "z")):
        held = lax.all_to_all(share_all, name, dim, dim, tiled=True)
        total = held[0]
        for i in range(1, held.shape[0]):
            total = total + held[i]
        share_all = total
    share_all = gather_sum(share_all, "agent")
    square_sum = jnp.sum(share_all * share_all).reshape(1, 1)
    square_sum = gather_sum(jnp.broadcast_to(square_sum, (1, 128)), TILE)[0, 0]
    factor = norm_limit / jnp.maximum(jnp.sqrt(square_sum), norm_limit)
    scaled = share_all * factor
    scaled = jnp.transpose(scaled, (1, 0, 2))
    return (d_feats, scaled[..., : 3 * channels], scaled[..., 3 * channels :])


def solution(mesh):
    agents_n, tiles = mesh.devices.shape
    cores = 2
    zs = min(8, tiles // cores)
    fine = Mesh(
        mesh.devices.reshape(agents_n, tiles // (cores * zs), zs, cores), ("agent",) + TILE
    )
    placed = (
        P("agent", TILE, None, None),
        P(),
        P(),
        P(),
        P(),
        P(),
        P("agent", TILE, None, None),
    )
    return jax.shard_map(
        body,
        mesh=fine,
        in_specs=placed,
        out_specs=(P("agent", TILE, None, None), P(None, TILE, None), P(None, TILE, None)),
        check_vma=False,
    )
```

```python
import functools
import math

import jax
import jax.numpy as jnp
from jax import lax
from jax.experimental import pallas as pl
from jax.sharding import Mesh, PartitionSpec as P

HEADS = 8
TILE = ("x2", "x1", "z4", "z2", "z1", "core")
MAXOFF = 2


def axis_bits(axis):
    count = lax.axis_size(axis)
    bits = count.bit_length() - 1
    assert 1 << bits == count
    return bits


def xor_pairs(count, bit):
    return [(i, i ^ (1 << bit)) for i in range(count)]


def tile_bit_order(count):
    bits = count.bit_length() - 1
    preferred = [0, 1, 4, 2, 5, 3]
    return [b for b in preferred if b < bits] + [b for b in range(bits) if b not in preferred]


def tile_twins(count):
    bits = count.bit_length() - 1
    pairs = {1: 4, 4: 1, 2: 5, 5: 2}
    return {b: t for b, t in pairs.items() if b < bits and t < bits}


def halving_sum(pieces, axis, bit_order, twins, keep_bits=False):
    count = lax.axis_size(axis)
    me = lax.axis_index(axis)
    bits = axis_bits(axis)
    rest = pieces.shape[1:]
    odd = (me & 1) == 1
    x = pieces.reshape((2,) * bits + rest)
    for step, bit in enumerate(bit_order):
        if step == 1 and twins:
            order = list(range(x.ndim))
            for b, t in twins.items():
                order[bits - 1 - b] = bits - 1 - t
            x = jnp.where(odd, jnp.transpose(x, order), x)
        twin = twins.get(bit, bit) if step > 0 else bit
        dim = bits - 1 - bit
        mine = jnp.where(odd, (me >> twin) & 1, (me >> bit) & 1)
        low = lax.index_in_dim(x, 0, dim, keepdims=True)
        high = lax.index_in_dim(x, 1, dim, keepdims=True)
        keep = jnp.where(mine == 1, high, low)
        send = jnp.where(mine == 1, low, high)
        pairs = [(i, i ^ (1 << (twin if i & 1 else bit))) for i in range(count)]
        x = keep + lax.ppermute(send, axis, pairs)
    return x if keep_bits else x.reshape(rest)


def gather_sum(x, axis):
    count = lax.axis_size(axis)
    copies = jnp.broadcast_to(x[None], (count,) + x.shape)
    held = lax.all_to_all(copies, axis, 0, 0, tiled=True)
    total = held[0]
    for i in range(1, count):
        total = total + held[i]
    return total


def doubling_sum(x, axis, bit_order):
    count = lax.axis_size(axis)
    for bit in bit_order:
        x = x + lax.ppermute(x, axis, xor_pairs(count, bit))
    return x


def with_halo(cells, sides, width):
    for axis, dim in sides:
        count = lax.axis_size(axis)
        ends = count - 1
        head = lax.slice_in_dim(cells, 0, width, axis=dim)
        tail = lax.slice_in_dim(cells, cells.shape[dim] - width, cells.shape[dim], axis=dim)
        cells = jnp.concatenate(
            [
                lax.ppermute(tail, axis, [(i, (i + 1) % count) for i in range(ends)]),
                cells,
                lax.ppermute(head, axis, [((i + 1) % count, i) for i in range(ends)]),
            ],
            axis=dim,
        )
    return cells


def relocate(rimmed, offsets, direction):
    padded = jnp.pad(rimmed, ((0, 0), (0, 0), (MAXOFF, MAXOFF), (0, 0)))
    row_count = rimmed.shape[1] - 2 * MAXOFF
    col_count = rimmed.shape[2]

    def pick_one(plane, offset):
        row_start = MAXOFF + direction * offset[0]
        col_start = MAXOFF + direction * offset[1]
        return lax.dynamic_slice(
            plane, (row_start, col_start, jnp.int32(0)), (row_count, col_count, plane.shape[2])
        )

    return jax.vmap(pick_one)(padded, offsets)


def attention_kernel(block_size, valid_ref, qkv_ref, da_ref, att_ref, split_ref):
    f32 = jnp.float32
    bf16 = jnp.bfloat16
    cells, agents, channels = da_ref.shape
    head_size = channels // HEADS
    blocks = agents // block_size
    rows = blocks * HEADS * block_size
    scale = head_size ** (-0.5)
    dims_nt = (((1,), (1,)), ((), ()))
    dims_tn = (((0,), (0,)), ((), ()))
    lane = lax.broadcasted_iota(jnp.int32, (HEADS, channels), 1)
    head = lax.broadcasted_iota(jnp.int32, (HEADS, channels), 0)
    head_mask = (lane // head_size == head).astype(f32).reshape(1, HEADS, 1, channels)
    row_id = lax.broadcasted_iota(jnp.int32, (rows, agents), 0)
    col_id = lax.broadcasted_iota(jnp.int32, (rows, agents), 1)
    row_agent = (row_id // (HEADS * block_size)) * block_size + row_id % block_size
    allowed = (valid_ref[...] > 0.5) | (row_agent == col_id)

    def stack(x):
        spread = x.astype(f32).reshape(blocks, 1, block_size, channels) * head_mask
        return spread.reshape(rows, channels).astype(bf16)

    def unstack(y):
        return jnp.sum(y.reshape(blocks, HEADS, block_size, channels) * head_mask, axis=1).reshape(
            agents, channels
        )

    def one_cell(c, carry):
        q = qkv_ref[c, :, 0:channels]
        k = qkv_ref[c, :, channels : 2 * channels]
        v = qkv_ref[c, :, 2 * channels : 3 * channels]
        q_rows = stack(q)
        da_rows = stack(da_ref[c])
        scores = lax.dot_general(q_rows, k, dims_nt, preferred_element_type=f32) * scale
        raised = jnp.where(allowed, jnp.exp(scores), f32(0.0))
        prob = raised / jnp.sum(raised, axis=1, keepdims=True)
        prob_low = prob.astype(bf16)
        att = unstack(jnp.dot(prob_low, v, preferred_element_type=f32))
        att_ref[c] = att.astype(bf16)
        prob_grad = lax.dot_general(da_rows, v, dims_nt, preferred_element_type=f32)
        score_grad = (
            prob * (prob_grad - jnp.sum(prob * prob_grad, axis=1, keepdims=True)) * scale
        ).astype(bf16)
        d_q = unstack(jnp.dot(score_grad, k, preferred_element_type=f32)).astype(bf16).astype(f32)
        d_k = jnp.zeros((agents, channels), f32)
        d_v = jnp.zeros((agents, channels), f32)
        for n in range(blocks):
            part = slice(n * HEADS * block_size, (n + 1) * HEADS * block_size)
            d_k = d_k + lax.dot_general(
                score_grad[part], q_rows[part], dims_tn, preferred_element_type=f32
            ).astype(bf16).astype(f32)
            d_v = d_v + lax.dot_general(
                prob_low[part], da_rows[part], dims_tn, preferred_element_type=f32
            ).astype(bf16).astype(f32)
        for i, d in enumerate((d_q, d_k, d_v)):
            hi = d.astype(bf16)
            split_ref[0, c, :, i * channels : (i + 1) * channels] = hi
            split_ref[1, c, :, i * channels : (i + 1) * channels] = (d - hi.astype(f32)).astype(bf16)
        return carry

    lax.fori_loop(0, cells, one_cell, 0)


def cell_attention(valid_row, qkv, d_attended, block_size):
    cells, agents, channels = d_attended.shape
    step = 4 if cells % 4 == 0 else 1
    return pl.pallas_call(
        functools.partial(attention_kernel, block_size),
        grid=(cells // step,),
        in_specs=[
            pl.BlockSpec((1, agents), lambda i: (0, 0)),
            pl.BlockSpec((step, agents, 3 * channels), lambda i: (i, 0, 0)),
            pl.BlockSpec((step, agents, channels), lambda i: (i, 0, 0)),
        ],
        out_specs=[
            pl.BlockSpec((step, agents, channels), lambda i: (i, 0, 0)),
            pl.BlockSpec((2, step, agents, 3 * channels), lambda i: (0, i, 0, 0)),
        ],
        out_shape=[
            jax.ShapeDtypeStruct((cells, agents, channels), jnp.bfloat16),
            jax.ShapeDtypeStruct((2, cells, agents, 3 * channels), jnp.bfloat16),
        ],
        cost_estimate=pl.CostEstimate(
            flops=cells * 48 * agents * HEADS * agents * channels,
            transcendentals=cells * agents * HEADS * agents,
            bytes_accessed=cells * agents * channels * 2 * 11,
        ),
    )(valid_row, qkv, d_attended)


def body(TILE, feats, types, valid, offsets, w_qkv, w_out, d_out):
    f32 = jnp.float32
    bf16 = jnp.bfloat16
    highest = lax.Precision.HIGHEST
    own_count, row_count, col_count, channels = feats.shape
    agents = own_count * lax.axis_size("agent")
    first_agent = lax.axis_index("agent") * own_count
    own_offsets = lax.dynamic_slice_in_dim(offsets, first_agent, own_count, 0)
    rimmed = with_halo(feats, ((TILE, 1),), MAXOFF)
    warped = relocate(rimmed, own_offsets, 1)
    cell_count = row_count * col_count
    head_size = channels // HEADS
    score_scale = head_size ** (-0.5)
    all_hot = (types[:, None] == jnp.arange(2)[None, :]).astype(bf16)
    flat_feats = warped.reshape(own_count, cell_count, channels)
    flat_grads = d_out.reshape(own_count, cell_count, channels)
    both = lax.all_to_all(
        jnp.concatenate([flat_feats, flat_grads], axis=-1),
        "agent",
        split_axis=1,
        concat_axis=0,
        tiled=True,
    )
    all_feats, all_grads = both[..., :channels], both[..., channels:]
    part_cells = all_feats.shape[1]
    pairs = agents * part_cells
    is_type1 = (types == 1)[None, :, None]
    type_mask = jnp.stack([types == 0, types == 1], axis=0)[:, None, :, None]
    feats_cm = jnp.transpose(all_feats, (1, 0, 2))
    grads_cm = jnp.transpose(all_grads, (1, 0, 2))
    qkv_both = jnp.einsum(
        "gac,tce->tgae", feats_cm, w_qkv, preferred_element_type=f32
    ).astype(bf16)
    qkv = jnp.where(is_type1, qkv_both[1], qkv_both[0])
    d_att_both = jnp.einsum(
        "gae,tce->tgac", grads_cm, w_out, preferred_element_type=f32
    ).astype(bf16)
    d_attended = jnp.where(is_type1, d_att_both[1], d_att_both[0])
    valid_row = (valid == 1).astype(f32).reshape(1, agents)
    attended, d_split = cell_attention(valid_row, qkv, d_attended, own_count)
    attended_typed = jnp.where(type_mask, attended[None], jnp.zeros((), bf16))
    raw_out = jnp.einsum(
        "tgac,gae->cte", attended_typed, grads_cm, preferred_element_type=f32
    )
    d_part_terms = jnp.einsum(
        "sgae,tce->stgac", d_split, w_qkv, preferred_element_type=f32
    )
    d_part_sum = d_part_terms[0] + d_part_terms[1]
    d_part = jnp.where(is_type1, d_part_sum[1], d_part_sum[0]).astype(bf16)
    d_part = jnp.transpose(d_part, (1, 0, 2))
    returned = lax.all_to_all(d_part, "agent", split_axis=0, concat_axis=1, tiled=True)
    d_warped = returned.reshape(own_count, row_count, col_count, channels)
    feats_typed = jnp.where(type_mask, feats_cm[None], jnp.zeros((), bf16))
    qkv_terms = jnp.einsum(
        "tgac,sgae->scte", feats_typed, d_split, preferred_element_type=f32
    )
    raw_qkv = qkv_terms[0] + qkv_terms[1]
    rimmed_grad = with_halo(d_warped, ((TILE, 1),), MAXOFF)
    d_feats = relocate(rimmed_grad, own_offsets, -1)
    norm_limit = math.sqrt(8.0 * channels * channels)
    raw_all = jnp.concatenate([raw_qkv, raw_out], axis=-1)
    tiles = lax.axis_size(TILE)
    share_rows = channels // tiles
    pieces = raw_all.reshape(tiles, share_rows, 2, 4 * channels)
    order = tile_bit_order(tiles)
    twins = tile_twins(tiles)
    head = order[:3]
    tail = sorted(order[3:], reverse=True)
    share_all = halving_sum(pieces, TILE, head, twins, keep_bits=True)
    if tail:
        bits = axis_bits(TILE)
        odd = (lax.axis_index(TILE) & 1) == 1
        back = list(range(share_all.ndim))
        for b, t in twins.items():
            back[bits - 1 - b] = bits - 1 - t
        share_all = jnp.where(odd, jnp.transpose(share_all, back), share_all)
        share_all = share_all.reshape((1 << len(tail),) + pieces.shape[1:])
        held = lax.all_to_all(share_all, tuple(TILE[len(TILE) - 1 - b] for b in tail), 0, 0, tiled=True)
        total = held[0]
        for i in range(1, held.shape[0]):
            total = total + held[i]
        share_all = total
    else:
        share_all = share_all.reshape(pieces.shape[1:])
    share_all = gather_sum(share_all, "agent")
    square_sum = jnp.sum(share_all * share_all).reshape(1, 1)
    square_sum = gather_sum(jnp.broadcast_to(square_sum, (1, 128)), TILE)[0, 0]
    factor = norm_limit / jnp.maximum(jnp.sqrt(square_sum), norm_limit)
    scaled = share_all * factor
    scaled = jnp.transpose(scaled, (1, 0, 2))
    return (d_feats, scaled[..., : 3 * channels], scaled[..., 3 * channels :])


def solution(mesh):
    agents_n, tiles = mesh.devices.shape
    bits = tiles.bit_length() - 1
    names = TILE[len(TILE) - bits :]
    fine = Mesh(mesh.devices.reshape((agents_n,) + (2,) * bits), ("agent",) + names)
    tile = names
    placed = (
        P("agent", tile, None, None),
        P(),
        P(),
        P(),
        P(),
        P(),
        P("agent", tile, None, None),
    )
    return jax.shard_map(
        functools.partial(body, tile),
        mesh=fine,
        in_specs=placed,
        out_specs=(P("agent", tile, None, None), P(None, tile, None), P(None, tile, None)),
        check_vma=False,
    )
```

```python
import functools
import math

import jax
import jax.numpy as jnp
from jax import lax
from jax.experimental import pallas as pl
from jax.sharding import PartitionSpec as P

HEADS = 8
MAXOFF = 2


def axis_bits(axis):
    count = lax.axis_size(axis)
    bits = count.bit_length() - 1
    assert 1 << bits == count
    return bits


def xor_pairs(count, bit):
    return [(i, i ^ (1 << bit)) for i in range(count)]


def tile_bit_order(count):
    bits = count.bit_length() - 1
    preferred = [0, 1, 4, 2, 5, 3]
    return [b for b in preferred if b < bits] + [b for b in range(bits) if b not in preferred]


def tile_twins(count):
    bits = count.bit_length() - 1
    pairs = {1: 4, 4: 1, 2: 5, 5: 2}
    return {b: t for b, t in pairs.items() if b < bits and t < bits}


def halving_sum(pieces, axis, bit_order, twins):
    count = lax.axis_size(axis)
    me = lax.axis_index(axis)
    bits = axis_bits(axis)
    rest = pieces.shape[1:]
    odd = (me & 1) == 1
    x = pieces.reshape((2,) * bits + rest)
    for step, bit in enumerate(bit_order):
        if step == 1 and twins:
            order = list(range(x.ndim))
            for b, t in twins.items():
                order[bits - 1 - b] = bits - 1 - t
            x = jnp.where(odd, jnp.transpose(x, order), x)
        twin = twins.get(bit, bit) if step > 0 else bit
        dim = bits - 1 - bit
        mine = jnp.where(odd, (me >> twin) & 1, (me >> bit) & 1)
        low = lax.index_in_dim(x, 0, dim, keepdims=True)
        high = lax.index_in_dim(x, 1, dim, keepdims=True)
        keep = jnp.where(mine == 1, high, low)
        send = jnp.where(mine == 1, low, high)
        pairs = [(i, i ^ (1 << (twin if i & 1 else bit))) for i in range(count)]
        x = keep + lax.ppermute(send, axis, pairs)
    return x.reshape(rest)


def gather_sum(x, axis):
    count = lax.axis_size(axis)
    copies = jnp.broadcast_to(x[None], (count,) + x.shape)
    held = lax.all_to_all(copies, axis, 0, 0, tiled=True)
    total = held[0]
    for i in range(1, count):
        total = total + held[i]
    return total


def doubling_sum(x, axis, bit_order):
    count = lax.axis_size(axis)
    for bit in bit_order:
        x = x + lax.ppermute(x, axis, xor_pairs(count, bit))
    return x


def with_halo(cells, sides, width):
    for axis, dim in sides:
        count = lax.axis_size(axis)
        ends = count - 1
        head = lax.slice_in_dim(cells, 0, width, axis=dim)
        tail = lax.slice_in_dim(cells, cells.shape[dim] - width, cells.shape[dim], axis=dim)
        cells = jnp.concatenate(
            [
                lax.ppermute(tail, axis, [(i, (i + 1) % count) for i in range(ends)]),
                cells,
                lax.ppermute(head, axis, [((i + 1) % count, i) for i in range(ends)]),
            ],
            axis=dim,
        )
    return cells


def relocate(rimmed, offsets, direction):
    padded = jnp.pad(rimmed, ((0, 0), (0, 0), (MAXOFF, MAXOFF), (0, 0)))
    row_count = rimmed.shape[1] - 2 * MAXOFF
    col_count = rimmed.shape[2]

    def pick_one(plane, offset):
        row_start = MAXOFF + direction * offset[0]
        col_start = MAXOFF + direction * offset[1]
        return lax.dynamic_slice(
            plane, (row_start, col_start, jnp.int32(0)), (row_count, col_count, plane.shape[2])
        )

    return jax.vmap(pick_one)(padded, offsets)


def attention_kernel(block_size, valid_ref, qkv_ref, da_ref, att_ref, split_ref):
    f32 = jnp.float32
    bf16 = jnp.bfloat16
    cells, agents, channels = da_ref.shape
    head_size = channels // HEADS
    blocks = agents // block_size
    rows = blocks * HEADS * block_size
    scale = head_size ** (-0.5)
    dims_nt = (((1,), (1,)), ((), ()))
    dims_tn = (((0,), (0,)), ((), ()))
    lane = lax.broadcasted_iota(jnp.int32, (HEADS, channels), 1)
    head = lax.broadcasted_iota(jnp.int32, (HEADS, channels), 0)
    head_mask = (lane // head_size == head).astype(f32).reshape(1, HEADS, 1, channels)
    row_id = lax.broadcasted_iota(jnp.int32, (rows, agents), 0)
    col_id = lax.broadcasted_iota(jnp.int32, (rows, agents), 1)
    row_agent = (row_id // (HEADS * block_size)) * block_size + row_id % block_size
    allowed = (valid_ref[...] > 0.5) | (row_agent == col_id)

    def stack(x):
        spread = x.astype(f32).reshape(blocks, 1, block_size, channels) * head_mask
        return spread.reshape(rows, channels).astype(bf16)

    def unstack(y):
        return jnp.sum(y.reshape(blocks, HEADS, block_size, channels) * head_mask, axis=1).reshape(
            agents, channels
        )

    def one_cell(c, carry):
        q = qkv_ref[c, :, 0:channels]
        k = qkv_ref[c, :, channels : 2 * channels]
        v = qkv_ref[c, :, 2 * channels : 3 * channels]
        q_rows = stack(q)
        da_rows = stack(da_ref[c])
        scores = lax.dot_general(q_rows, k, dims_nt, preferred_element_type=f32) * scale
        raised = jnp.where(allowed, jnp.exp(scores), f32(0.0))
        prob = raised / jnp.sum(raised, axis=1, keepdims=True)
        prob_low = prob.astype(bf16)
        att = unstack(jnp.dot(prob_low, v, preferred_element_type=f32))
        att_ref[c] = att.astype(bf16)
        prob_grad = lax.dot_general(da_rows, v, dims_nt, preferred_element_type=f32)
        score_grad = (
            prob * (prob_grad - jnp.sum(prob * prob_grad, axis=1, keepdims=True)) * scale
        ).astype(bf16)
        d_q = unstack(jnp.dot(score_grad, k, preferred_element_type=f32)).astype(bf16).astype(f32)
        d_k = jnp.zeros((agents, channels), f32)
        d_v = jnp.zeros((agents, channels), f32)
        for n in range(blocks):
            part = slice(n * HEADS * block_size, (n + 1) * HEADS * block_size)
            d_k = d_k + lax.dot_general(
                score_grad[part], q_rows[part], dims_tn, preferred_element_type=f32
            ).astype(bf16).astype(f32)
            d_v = d_v + lax.dot_general(
                prob_low[part], da_rows[part], dims_tn, preferred_element_type=f32
            ).astype(bf16).astype(f32)
        for i, d in enumerate((d_q, d_k, d_v)):
            hi = d.astype(bf16)
            split_ref[0, c, :, i * channels : (i + 1) * channels] = hi
            split_ref[1, c, :, i * channels : (i + 1) * channels] = (d - hi.astype(f32)).astype(bf16)
        return carry

    lax.fori_loop(0, cells, one_cell, 0)


def cell_attention(valid_row, qkv, d_attended, block_size):
    cells, agents, channels = d_attended.shape
    step = 4 if cells % 4 == 0 else 1
    return pl.pallas_call(
        functools.partial(attention_kernel, block_size),
        grid=(cells // step,),
        in_specs=[
            pl.BlockSpec((1, agents), lambda i: (0, 0)),
            pl.BlockSpec((step, agents, 3 * channels), lambda i: (i, 0, 0)),
            pl.BlockSpec((step, agents, channels), lambda i: (i, 0, 0)),
        ],
        out_specs=[
            pl.BlockSpec((step, agents, channels), lambda i: (i, 0, 0)),
            pl.BlockSpec((2, step, agents, 3 * channels), lambda i: (0, i, 0, 0)),
        ],
        out_shape=[
            jax.ShapeDtypeStruct((cells, agents, channels), jnp.bfloat16),
            jax.ShapeDtypeStruct((2, cells, agents, 3 * channels), jnp.bfloat16),
        ],
        cost_estimate=pl.CostEstimate(
            flops=cells * 48 * agents * HEADS * agents * channels,
            transcendentals=cells * agents * HEADS * agents,
            bytes_accessed=cells * agents * channels * 2 * 11,
        ),
    )(valid_row, qkv, d_attended)


def body(feats, types, valid, offsets, w_qkv, w_out, d_out):
    f32 = jnp.float32
    bf16 = jnp.bfloat16
    highest = lax.Precision.HIGHEST
    own_count, row_count, col_count, channels = feats.shape
    agents = own_count * lax.axis_size("agent")
    first_agent = lax.axis_index("agent") * own_count
    own_offsets = lax.dynamic_slice_in_dim(offsets, first_agent, own_count, 0)
    rimmed = with_halo(feats, (("tile", 1),), MAXOFF)
    warped = relocate(rimmed, own_offsets, 1)
    cell_count = row_count * col_count
    head_size = channels // HEADS
    score_scale = head_size ** (-0.5)
    all_hot = (types[:, None] == jnp.arange(2)[None, :]).astype(bf16)
    flat_feats = warped.reshape(own_count, cell_count, channels)
    flat_grads = d_out.reshape(own_count, cell_count, channels)
    both = lax.all_to_all(
        jnp.concatenate([flat_feats, flat_grads], axis=-1),
        "agent",
        split_axis=1,
        concat_axis=0,
        tiled=True,
    )
    all_feats, all_grads = both[..., :channels], both[..., channels:]
    part_cells = all_feats.shape[1]
    pairs = agents * part_cells
    is_type1 = (types == 1)[None, :, None]
    type_mask = jnp.stack([types == 0, types == 1], axis=0)[:, None, :, None]
    feats_cm = jnp.transpose(all_feats, (1, 0, 2))
    grads_cm = jnp.transpose(all_grads, (1, 0, 2))
    qkv_both = jnp.einsum(
        "gac,tce->tgae", feats_cm, w_qkv, preferred_element_type=f32
    ).astype(bf16)
    qkv = jnp.where(is_type1, qkv_both[1], qkv_both[0])
    d_att_both = jnp.einsum(
        "gae,tce->tgac", grads_cm, w_out, preferred_element_type=f32
    ).astype(bf16)
    d_attended = jnp.where(is_type1, d_att_both[1], d_att_both[0])
    valid_row = (valid == 1).astype(f32).reshape(1, agents)
    attended, d_split = cell_attention(valid_row, qkv, d_attended, own_count)
    attended_typed = jnp.where(type_mask, attended[None], jnp.zeros((), bf16))
    raw_out = jnp.einsum(
        "tgac,gae->cte", attended_typed, grads_cm, preferred_element_type=f32
    )
    d_part_terms = jnp.einsum(
        "sgae,tce->stgac", d_split, w_qkv, preferred_element_type=f32
    )
    d_part_sum = d_part_terms[0] + d_part_terms[1]
    d_part = jnp.where(is_type1, d_part_sum[1], d_part_sum[0]).astype(bf16)
    d_part = jnp.transpose(d_part, (1, 0, 2))
    returned = lax.all_to_all(d_part, "agent", split_axis=0, concat_axis=1, tiled=True)
    d_warped = returned.reshape(own_count, row_count, col_count, channels)
    feats_typed = jnp.where(type_mask, feats_cm[None], jnp.zeros((), bf16))
    qkv_terms = jnp.einsum(
        "tgac,sgae->scte", feats_typed, d_split, preferred_element_type=f32
    )
    raw_qkv = qkv_terms[0] + qkv_terms[1]
    rimmed_grad = with_halo(d_warped, (("tile", 1),), MAXOFF)
    d_feats = relocate(rimmed_grad, own_offsets, -1)
    norm_limit = math.sqrt(8.0 * channels * channels)
    raw_all = jnp.concatenate([raw_qkv[:, 0], raw_out[:, 0], raw_qkv[:, 1], raw_out[:, 1]], axis=-1)
    tiles = lax.axis_size("tile")
    share_rows = channels // tiles
    pieces = raw_all.reshape(tiles, share_rows, 2 * 4 * channels)
    share_all = halving_sum(pieces, "tile", tile_bit_order(tiles), tile_twins(tiles))
    share_all = gather_sum(share_all, "agent")
    square_sum = jnp.sum(share_all * share_all).reshape(1, 1)
    square_sum = gather_sum(jnp.broadcast_to(square_sum, (1, 128)), "tile")[0, 0]
    factor = norm_limit / jnp.maximum(jnp.sqrt(square_sum), norm_limit)
    scaled = share_all * factor
    scaled = jnp.transpose(scaled.reshape(share_rows, 2, 4 * channels), (1, 0, 2))
    return (d_feats, scaled[..., : 3 * channels], scaled[..., 3 * channels :])


def solution(mesh):
    placed = (
        P("agent", "tile", None, None),
        P(),
        P(),
        P(),
        P(),
        P(),
        P("agent", "tile", None, None),
    )
    return jax.shard_map(
        body,
        mesh=mesh,
        in_specs=placed,
        out_specs=(P("agent", "tile", None, None), P(None, "tile", None), P(None, "tile", None)),
        check_vma=False,
    )
```
